32 devices in a mesh: grp: 1, node: 8 (over z, y), dev: 4 (over x, core).
Axes of the slice: x: 2, y: 2, z: 4, core: 2. Of those that a mesh axis runs over, the one named last changes fastest.
Arguments:
- query_latent: bfloat16 [32, 128, 512], P(('grp', 'node', 'dev')), may hold values from -35 to 35
- query_rope: bfloat16 [32, 8192], P(('grp', 'node', 'dev')), may hold values from -5 to 5
- latent_cache: bfloat16 [32, 256, 512], P(('grp', 'node', 'dev')), may hold values from -5 to 5
- rope_cache: bfloat16 [32, 64, 256], P(('grp', 'node', 'dev')), may hold values from -5 to 5
- lengths: int32 [32], P(('grp', 'node', 'dev')), may hold values from 2 to 256, as said below
- moe_input: bfloat16 [32, 7168], P(('grp', 'node', 'dev')), may hold values from -6 to 6
- routes: int32 [32, 8], P(('grp', 'node', 'dev')), may hold values from 0 to 15, all different within a row; in each aligned block of 4 rows (0 to 3, 4 to 7, ...) at most 2 rows name the same one
- route_weight: bfloat16 [32, 8], P(('grp', 'node', 'dev')), may hold values from 0.029907227 to 0.29882812
- gate_weight: bfloat16 [32, 7168, 1024], P(('node', 'dev')), may hold values from -0.0625 to 0.0625
- up_weight: bfloat16 [32, 7168, 1024], P(('node', 'dev')), may hold values from -0.0625 to 0.0625
- down_weight: bfloat16 [32, 1024, 7168], P(('node', 'dev')), may hold values from -0.125 to 0.125
Outputs:
- attended: bfloat16 [32, 128, 512], P(('grp', 'node', 'dev'))
- moe_output: bfloat16 [32, 7168], P(('grp', 'node', 'dev'))
The draws below stay inside these ranges and needn't reach their ends.
Inputs may be any that keep to these rules, and one draw needn't show every extreme that they name: `routes`: each row names 8 different experts; in each aligned block of 4 rows every expert is named by exactly 2 rows. `lengths`: every request has at least two live positions; in every draw some request has all 256.
All inputs are finite; a program needn't handle non-finite values.
Results may differ from the reference program's by a relative error of at most 0.0085.
Values may be sent and summed in bfloat16 or wider, within the bound.
No kernel may reach another device: no remote copies, remote signals or barrier semaphores. Data moves between devices by JAX's collectives and lax.ppermute only.
A program may use at most 128 MiB of HBM per device.

```python
import math
import jax
import jax.numpy as jnp
import numpy as np
from jax import lax

D = 7168
FF = 2048
HEADS = 128
LATENT = 512
ROPE = 64
TOPK = 8
CTX = 256
ROW_DEV = 1
SPLIT = 2
FF_DEV = 1024
EXPERTS = 16
MOST = 2
ROWS = 32
REQS = 32
N_GRP = 1
N_NODE = 8
N_DEV = 4


def first_latent(key):
    values = jax.random.normal(jax.random.fold_in(key, 13), (REQS, 1, LATENT), jnp.float32)
    return jnp.clip(values, -5.0, 5.0)


def first_rope(key):
    values = jax.random.normal(jax.random.fold_in(key, 14), (REQS, ROPE, 1), jnp.float32)
    return jnp.clip(values, -5.0, 5.0)


def draw_latent_cache(key, part):
    leading = first_latent(key)
    others = jnp.clip(jax.random.normal(jax.random.fold_in(key, 11), (REQS, CTX, LATENT), jnp.float32), -5.0, 5.0)
    position = jnp.arange(CTX, dtype=jnp.int32).reshape(1, CTX, 1)
    cache = jnp.where(position == 0, leading, others)
    return cache.astype(jnp.bfloat16)


def draw_rope_cache(key, part):
    leading = first_rope(key)
    others = jnp.clip(jax.random.normal(jax.random.fold_in(key, 15), (REQS, ROPE, CTX), jnp.float32), -5.0, 5.0)
    position = jnp.arange(CTX, dtype=jnp.int32).reshape(1, 1, CTX)
    cache = jnp.where(position == 0, leading, others)
    return cache.astype(jnp.bfloat16)


def draw_query_latent(key, part):
    values = jnp.clip(jax.random.normal(jax.random.fold_in(key, 12), (REQS, HEADS, LATENT), jnp.float32), -5.0, 5.0)
    return values.astype(jnp.bfloat16)


def draw_query_rope(key, part):
    values = jnp.clip(jax.random.normal(jax.random.fold_in(key, 16), (REQS, HEADS * ROPE), jnp.float32), -5.0, 5.0)
    return values.astype(jnp.bfloat16)


def draw_lengths(key, part):
    earlier = jax.random.randint(jax.random.fold_in(key, 21), (REQS,), 0, CTX, jnp.int32)
    later = jax.random.randint(jax.random.fold_in(key, 22), (REQS,), 0, CTX, jnp.int32)
    counts = jnp.maximum(jnp.minimum(earlier, later) + 1, 2)
    chosen = jax.random.randint(jax.random.fold_in(key, 23), (), 0, REQS, jnp.int32)
    return jnp.where(jnp.arange(REQS, dtype=jnp.int32) == chosen, CTX, counts).astype(jnp.int32)


def block_levels(key, dims, cuts, low, high):
    def one(axis_at, blocks):
        heights = jax.random.uniform(jax.random.fold_in(jax.random.fold_in(key, 6), axis_at), (blocks,), jnp.float32, low / len(cuts), high / len(cuts))
        return jnp.repeat(jnp.exp(heights), dims[axis_at] // blocks).reshape((-1,) + (1,) * (len(dims) - axis_at - 1))

    loudness = one(*cuts[0])
    for cut in cuts[1:]:
        loudness = loudness * one(*cut)
    return loudness


def deal_out(stream_key, own, number, rows, number_of, top, most, lean):
    sequence = jax.random.permutation(stream_key, number_of)
    packed, ordinary = portions_of(number_of, rows * top, most, lean, True), portions_of(number_of, rows * top, most, lean, False)
    places = jnp.arange(number_of)

    def named(sizes, rotation):
        used = int((sizes > 0).sum())
        fixed = max(1, used // 4)
        passed = fixed + (places - fixed + rotation * (used - fixed)) % max(1, number_of - fixed)
        return jnp.zeros((number_of,), jnp.int32).at[sequence[jnp.where(places < fixed, places, passed)]].set(jnp.asarray(sizes, jnp.int32))

    sizes = jnp.where(number % 4 == 0, named(packed, number // 4), named(ordinary, number - number // 4 - 1))
    mixed = jax.random.permutation(jax.random.fold_in(own, 3), number_of)
    donor, sink = mixed[0:number_of // 2 * 2:2], mixed[1:number_of // 2 * 2:2]
    room = jnp.minimum(sizes[donor] - 1, most - sizes[sink]) // 2
    room = jnp.where((donor == sequence[0]) | (sink == sequence[0]) | (sizes[sink] == 0), 0, jnp.maximum(room, 0))
    passed = jax.random.randint(jax.random.fold_in(own, 4), (number_of // 2,), 0, 1 << 20) % (room + 1)
    sizes = sizes.at[donor].add(-passed).at[sink].add(passed)
    members = jnp.searchsorted(jnp.cumsum(sizes), jnp.arange(rows * top), side="right").astype(jnp.int32)
    table = members.reshape(top, rows).T
    table = table[jax.random.permutation(jax.random.fold_in(own, 1), rows)]
    rotation = jax.random.randint(jax.random.fold_in(own, 2), (rows, 1), 0, top)
    return jnp.take_along_axis(table, (jnp.arange(top)[None, :] + rotation) % top, axis=1)


def portions_of(number_of, total, bound, skew, full):
    portions = [(1 << 20) // math.isqrt(standing ** skew) + 1 for standing in range(1, number_of + 1)]
    largest = bound if full else min(bound, max(-(-total // number_of), total * portions[0] // sum(portions)))
    least = 1 if total - largest >= number_of - 1 else 0
    given, spare = [largest] + [least] * (number_of - 1), total - largest - least * (number_of - 1)
    while spare > 0:
        candidates = [i for i in range(1, number_of) if given[i] < largest] or [i for i in range(1, number_of) if given[i] < bound]
        pool, remaining = sum([portions[i] for i in candidates]), spare
        for i in candidates:
            extra = min(bound - given[i], max(1, remaining * portions[i] // pool), spare)
            given[i] = given[i] + extra
            spare = spare - extra
    return np.array(given)


def bell_draw(stream_key, dims, spread, reach, cuts=(), kind=jnp.bfloat16):
    array = spread * jax.random.normal(stream_key, dims, jnp.float32)
    if cuts:
        array = array * block_levels(stream_key, dims, cuts, -0.22, 0.18)
    return jnp.clip(array, -reach, reach).astype(kind)


def setup_inputs(seed: int = 0) -> dict:
    arg_keys = jax.random.split(jax.random.key(seed), 12)
    query_latent = draw_query_latent(jax.random.fold_in(arg_keys[11], 71), 0)
    query_rope = draw_query_rope(jax.random.fold_in(arg_keys[11], 71), 0)
    latent_cache = draw_latent_cache(jax.random.fold_in(arg_keys[11], 71), 0)
    rope_cache = draw_rope_cache(jax.random.fold_in(arg_keys[11], 71), 0)
    lengths = draw_lengths(jax.random.fold_in(arg_keys[11], 71), 0)
    moe_input = bell_draw(arg_keys[5], (ROWS, D), 1.0, 6.0, ((0, 32),))
    routes_keys = jax.random.split(jax.random.fold_in(arg_keys[6], 1), ROWS // (N_DEV * ROW_DEV))
    routes_turns = jax.random.permutation(jax.random.fold_in(arg_keys[6], 3), ROWS // (N_DEV * ROW_DEV))
    routes = jax.vmap(lambda own, number: deal_out(jax.random.fold_in(arg_keys[6], 2), own, number, N_DEV * ROW_DEV, EXPERTS, TOPK, MOST, 0))(routes_keys, routes_turns).reshape((ROWS, TOPK))
    route_weight = jnp.clip(jnp.exp(math.log(0.29882812) - 2.30176843 * jax.random.uniform(arg_keys[7], (ROWS, TOPK), jnp.float32) ** block_levels(arg_keys[7], (ROWS, TOPK), ((0, 32),), -0.2, 0.2)), 0.029907227, 0.29882812).astype(jnp.bfloat16)
    gate_weight = bell_draw(arg_keys[8], (EXPERTS * SPLIT, D, FF_DEV), D ** -0.5, 0.0625, ((0, 32),))
    up_weight = bell_draw(arg_keys[9], (EXPERTS * SPLIT, D, FF_DEV), D ** -0.5, 0.0625, ((0, 32),))
    down_weight = bell_draw(arg_keys[10], (EXPERTS * SPLIT, FF_DEV, D), FF ** -0.5, 0.125, ((0, 32),))
    return {"query_latent": query_latent, "query_rope": query_rope, "latent_cache": latent_cache, "rope_cache": rope_cache, "lengths": lengths, "moe_input": moe_input, "routes": routes, "route_weight": route_weight, "gate_weight": gate_weight, "up_weight": up_weight, "down_weight": down_weight}


score_scale = 1.0 / math.sqrt(192.0)

def normalize(scores, usable):
    masked = jnp.where(usable, scores, -jnp.inf)
    largest = lax.optimization_barrier(jnp.max(masked, axis=-1, keepdims=True))
    powers = jnp.exp(masked - largest)
    return (powers / lax.optimization_barrier(jnp.sum(powers, axis=-1, keepdims=True))).astype(jnp.bfloat16)

def attend(query_latent, query_rope, latent_cache, rope_cache, lengths):
    requests = query_latent.shape[0]
    rope_query = query_rope.reshape(requests, HEADS, ROPE).astype(jnp.float32)
    latent_part = jnp.einsum('rhc,rtc->rht', query_latent.astype(jnp.float32), latent_cache.astype(jnp.float32))
    rope_part = jnp.einsum('rhk,rkt->rht', rope_query, rope_cache.astype(jnp.float32))
    scores = score_scale * (latent_part + rope_part)
    position = jnp.arange(CTX, dtype=jnp.int32)
    usable = position[None, None, :] < lengths[:, None, None]
    weights = normalize(scores, usable)
    output = jnp.einsum('rht,rtc->rhc', weights.astype(jnp.float32), latent_cache.astype(jnp.float32))
    return output.astype(jnp.bfloat16)

def experts(moe_input, routes, route_weight, gate_weight, up_weight, down_weight):
    feature_count = moe_input.shape[1]
    capacity = N_GRP * N_NODE * MOST

    def one_expert(accumulated, expert):
        matches = routes == expert
        chosen = jnp.any(matches, axis=1)
        picked = jnp.nonzero(chosen, size=capacity, fill_value=0)[0].astype(jnp.int32)
        weight = lax.optimization_barrier(jnp.sum(jnp.where(matches, route_weight.astype(jnp.float32), 0.0), axis=1))
        picked_rows = moe_input[picked]
        first_row = (expert * SPLIT).astype(jnp.int32)
        gate_rows = lax.dynamic_slice_in_dim(gate_weight, first_row, SPLIT, 0)
        up_rows = lax.dynamic_slice_in_dim(up_weight, first_row, SPLIT, 0)
        down_rows = lax.dynamic_slice_in_dim(down_weight, first_row, SPLIT, 0)
        gate_full = jnp.transpose(gate_rows, (1, 0, 2)).reshape(feature_count, SPLIT * FF_DEV)
        up_full = jnp.transpose(up_rows, (1, 0, 2)).reshape(feature_count, SPLIT * FF_DEV)
        gate_sum = jnp.dot(picked_rows, gate_full, preferred_element_type=jnp.float32)
        up_sum = jnp.dot(picked_rows, up_full, preferred_element_type=jnp.float32)
        hidden = (jax.nn.silu(gate_sum) * up_sum).astype(jnp.bfloat16).reshape(capacity, SPLIT, FF_DEV)
        slice_parts = jnp.einsum('rsf,sfd->rsd', hidden.astype(jnp.float32), down_rows.astype(jnp.float32))
        slice_parts = slice_parts.astype(jnp.bfloat16)
        output = lax.optimization_barrier(jnp.sum(slice_parts.astype(jnp.float32), axis=1))
        accumulated = accumulated.at[picked].add(weight[picked][:, None] * output)
        return (accumulated, None)
    start_value = jnp.zeros((moe_input.shape[0], feature_count), jnp.float32)
    accumulated = lax.scan(one_expert, start_value, jnp.arange(EXPERTS, dtype=jnp.int32))[0]
    return accumulated.astype(jnp.bfloat16)

def reference(query_latent, query_rope, latent_cache, rope_cache, lengths, moe_input, routes, route_weight, gate_weight, up_weight, down_weight):
    attended = attend(query_latent, query_rope, latent_cache, rope_cache, lengths)
    moe_output = experts(moe_input, routes, route_weight, gate_weight, up_weight, down_weight)
    return (attended, moe_output)
```

```python
import math

import jax
import jax.numpy as jnp
from jax import lax
from jax.sharding import PartitionSpec as P

E_NODE = 2


score_scale = 1.0 / math.sqrt(192.0)


def attention_scores(query_latent, rope_query, latent_block, rope_block):
    latent_part = jnp.einsum(
        "rhc,rtc->rht", query_latent, latent_block, preferred_element_type=jnp.float32
    )
    rope_part = jnp.einsum(
        "rhk,rkt->rht", rope_query, rope_block, preferred_element_type=jnp.float32
    )
    return score_scale * (latent_part + rope_part)


def normalize(scores, usable):
    masked = jnp.where(usable, scores, -jnp.inf)
    largest = jnp.max(masked, axis=-1, keepdims=True)
    powers = jnp.exp(masked - largest)
    return (powers / jnp.sum(powers, axis=-1, keepdims=True)).astype(jnp.bfloat16)


def attend(query_latent, query_rope, latent_cache, rope_cache, lengths):
    requests, head_count, latent = query_latent.shape
    context = latent_cache.shape[1]
    rope_query = query_rope.reshape(requests, head_count, -1)
    position = lax.broadcasted_iota(jnp.int32, (1, 1, context), 2)
    usable = position < lengths[:, None, None]
    block_width = min(128, context)
    blocks_live = (jnp.max(lengths) + block_width - 1) // block_width

    def score_block(counter, scores):
        block_start = counter * block_width
        latent_block = lax.dynamic_slice_in_dim(latent_cache, block_start, block_width, 1)
        rope_block = lax.dynamic_slice_in_dim(rope_cache, block_start, block_width, 2)
        block_scores = attention_scores(query_latent, rope_query, latent_block, rope_block)
        return lax.dynamic_update_slice_in_dim(scores, block_scores, block_start, 2)

    empty_scores = jnp.full((requests, head_count, context), -jnp.inf, jnp.float32)
    scores = lax.fori_loop(0, blocks_live, score_block, empty_scores)
    weights = normalize(scores, usable)

    def value_block(counter, accumulated):
        block_start = counter * block_width
        weight_block = lax.dynamic_slice_in_dim(weights, block_start, block_width, 2)
        latent_block = lax.dynamic_slice_in_dim(latent_cache, block_start, block_width, 1)
        return accumulated + jnp.einsum(
            "rht,rtc->rhc", weight_block, latent_block, preferred_element_type=jnp.float32
        )

    output = lax.fori_loop(
        0, blocks_live, value_block, jnp.zeros((requests, head_count, latent), jnp.float32)
    )
    return output.astype(jnp.bfloat16)


def shards(
    query_latent,
    query_rope,
    latent_cache,
    rope_cache,
    lengths,
    moe_input,
    routes,
    route_weight,
    gate_weight,
    up_weight,
    down_weight,
):
    attended = attend(query_latent, query_rope, latent_cache, rope_cache, lengths)
    feature_count = moe_input.shape[1]
    top = routes.shape[1]
    packed = jnp.concatenate(
        [moe_input, routes.astype(jnp.bfloat16), route_weight.astype(jnp.bfloat16)], axis=1
    )
    pool = lax.all_gather(packed, "dev", axis=0, tiled=True)
    pool_rows = pool[:, :feature_count]
    pool_routes = pool[:, feature_count : feature_count + top].astype(jnp.int32)
    pool_weights = pool[:, feature_count + top :]
    node_count = lax.axis_size("node")
    dev_count = lax.axis_size("dev")
    expert_half = lax.axis_index("dev") // (dev_count // E_NODE)
    pooled = pool_rows.shape[0]
    slot_count = pooled * pool_routes.shape[1] // (E_NODE * node_count)
    targets = jnp.arange(node_count, dtype=jnp.int32) * E_NODE + expert_half
    matches = pool_routes[:, :, None] == targets[None, None, :]
    chosen = jnp.sum(matches.astype(jnp.int32), axis=1)
    route_share = jnp.sum(
        jnp.where(matches, pool_weights[:, :, None].astype(jnp.float32), 0.0), axis=1
    )
    before = jnp.cumsum(chosen, axis=0) - chosen
    copies = 1
    per_copy = slot_count // copies
    slot_index = jnp.arange(slot_count, dtype=jnp.int32).reshape(1, copies, per_copy, 1)
    selection = (chosen.T[:, None, None, :] == 1) & (before.T[:, None, None, :] == slot_index)
    selector = selection.astype(jnp.bfloat16)
    weighted = (selection.astype(jnp.float32) * route_share.T[:, None, None, :]).astype(
        jnp.bfloat16
    )
    outgoing = jnp.einsum("ncsp,pd->cnsd", selector, pool_rows, preferred_element_type=jnp.float32)
    outgoing = outgoing.astype(jnp.bfloat16).reshape(copies * node_count, per_copy, feature_count)
    weighted, outgoing = (weighted, outgoing)
    arrived = lax.all_to_all(outgoing, "node", split_axis=0, concat_axis=0, tiled=True)
    peer_count, slot_total, width_total = arrived.shape
    flattened = arrived.reshape(peer_count * slot_total, width_total)
    gate_sum = jnp.dot(flattened, gate_weight[0], preferred_element_type=jnp.float32)
    up_sum = jnp.dot(flattened, up_weight[0], preferred_element_type=jnp.float32)
    hidden = (jax.nn.silu(gate_sum) * up_sum).astype(jnp.bfloat16)
    produced = jnp.dot(hidden, down_weight[0], preferred_element_type=jnp.float32).astype(
        jnp.bfloat16
    )
    partial_value = produced.reshape(peer_count, slot_total, width_total)
    returned = lax.all_to_all(partial_value, "node", split_axis=0, concat_axis=0, tiled=True)
    returned = returned.reshape(copies, node_count, slot_count // copies, feature_count)
    pool_sum = jnp.einsum("ncsp,cnsd->pd", weighted, returned, preferred_element_type=jnp.float32)
    if dev_count > 8:
        combined = lax.psum_scatter(pool_sum, "dev", scatter_dimension=0, tiled=True)
        return (attended, combined.astype(jnp.bfloat16))
    own = lax.axis_index("dev")
    rows_per = pooled // dev_count
    combined = lax.dynamic_slice_in_dim(pool_sum, own * rows_per, rows_per, 0)
    for shift in range(1, dev_count):
        target = (own + shift) % dev_count
        outgoing_part = lax.dynamic_slice_in_dim(pool_sum, target * rows_per, rows_per, 0)
        combined = combined + lax.ppermute(
            outgoing_part, "dev", [(i, (i + shift) % dev_count) for i in range(dev_count)]
        )
    return (attended, combined.astype(jnp.bfloat16))


def solution(mesh):
    in_specs = (
        P(("grp", "node", "dev"), None, None),
        P(("grp", "node", "dev"), None),
        P(("grp", "node", "dev"), None, None),
        P(("grp", "node", "dev"), None, None),
        P(("grp", "node", "dev")),
        P(("grp", "node", "dev"), None),
        P(("grp", "node", "dev"), None),
        P(("grp", "node", "dev"), None),
        P(("node", "dev"), None, None),
        P(("node", "dev"), None, None),
        P(("node", "dev"), None, None),
    )
    out_specs = (P(("grp", "node", "dev"), None, None), P(("grp", "node", "dev"), None))
    return jax.shard_map(shards, mesh=mesh, in_specs=in_specs, out_specs=out_specs, check_vma=False)
```

```python
import math

import jax
import jax.numpy as jnp
from jax import lax
from jax.experimental import pallas as pl
from jax.experimental.pallas import tpu as pltpu
from jax.sharding import PartitionSpec as P

E_NODE = 2


score_scale = 1.0 / math.sqrt(192.0)


def attention_scores(query_latent, rope_query, latent_block, rope_block):
    latent_part = jnp.einsum(
        "rhc,rtc->rht", query_latent, latent_block, preferred_element_type=jnp.float32
    )
    rope_part = jnp.einsum(
        "rhk,rkt->rht", rope_query, rope_block, preferred_element_type=jnp.float32
    )
    return score_scale * (latent_part + rope_part)


def expert_slice(tokens, gate_block, up_block, down_block):
    rows, feature_count = tokens.shape
    hidden_count = gate_block.shape[2]
    width = min(256, hidden_count)
    steps = hidden_count // width

    def kernel(x_ref, gate_ref, up_ref, down_ref, out_ref, acc_ref):
        step = pl.program_id(0)

        @pl.when(step == 0)
        def _():
            acc_ref[...] = jnp.zeros_like(acc_ref)

        x = x_ref[...]
        gate_sum = jnp.dot(x, gate_ref[...], preferred_element_type=jnp.float32)
        up_sum = jnp.dot(x, up_ref[...], preferred_element_type=jnp.float32)
        hidden = (gate_sum / (1.0 + jnp.exp(-gate_sum)) * up_sum).astype(jnp.bfloat16)
        acc_ref[...] += jnp.dot(hidden, down_ref[...], preferred_element_type=jnp.float32)

        @pl.when(step == steps - 1)
        def _():
            out_ref[...] = acc_ref[...].astype(out_ref.dtype)

    return pl.pallas_call(
        kernel,
        grid=(steps,),
        in_specs=[
            pl.BlockSpec((rows, feature_count), lambda j: (0, 0)),
            pl.BlockSpec((None, feature_count, width), lambda j: (0, 0, j)),
            pl.BlockSpec((None, feature_count, width), lambda j: (0, 0, j)),
            pl.BlockSpec((None, width, feature_count), lambda j: (0, j, 0)),
        ],
        out_specs=pl.BlockSpec((rows, feature_count), lambda j: (0, 0)),
        out_shape=jax.ShapeDtypeStruct((rows, feature_count), jnp.bfloat16),
        scratch_shapes=[pltpu.VMEM((rows, feature_count), jnp.float32)],
        compiler_params=pltpu.CompilerParams(
            dimension_semantics=("arbitrary",), vmem_limit_bytes=100 * 1024 * 1024
        ),
    )(tokens, gate_block, up_block, down_block)


def normalize(scores, usable):
    masked = jnp.where(usable, scores, -jnp.inf)
    largest = jnp.max(masked, axis=-1, keepdims=True)
    powers = jnp.exp(masked - largest)
    return (powers / jnp.sum(powers, axis=-1, keepdims=True)).astype(jnp.bfloat16)


def attend(query_latent, query_rope, latent_cache, rope_cache, lengths):
    requests, head_count, latent = query_latent.shape
    context = latent_cache.shape[1]
    rope_query = query_rope.reshape(requests, head_count, -1)
    position = lax.broadcasted_iota(jnp.int32, (1, 1, context), 2)
    usable = position < lengths[:, None, None]
    block_width = min(128, context)
    blocks_live = (jnp.max(lengths) + block_width - 1) // block_width

    def score_block(counter, scores):
        block_start = counter * block_width
        latent_block = lax.dynamic_slice_in_dim(latent_cache, block_start, block_width, 1)
        rope_block = lax.dynamic_slice_in_dim(rope_cache, block_start, block_width, 2)
        block_scores = attention_scores(query_latent, rope_query, latent_block, rope_block)
        return lax.dynamic_update_slice_in_dim(scores, block_scores, block_start, 2)

    empty_scores = jnp.full((requests, head_count, context), -jnp.inf, jnp.float32)
    scores = lax.fori_loop(0, blocks_live, score_block, empty_scores)
    weights = normalize(scores, usable)

    def value_block(counter, accumulated):
        block_start = counter * block_width
        weight_block = lax.dynamic_slice_in_dim(weights, block_start, block_width, 2)
        latent_block = lax.dynamic_slice_in_dim(latent_cache, block_start, block_width, 1)
        return accumulated + jnp.einsum(
            "rht,rtc->rhc", weight_block, latent_block, preferred_element_type=jnp.float32
        )

    output = lax.fori_loop(
        0, blocks_live, value_block, jnp.zeros((requests, head_count, latent), jnp.float32)
    )
    return output.astype(jnp.bfloat16)


def shards(
    query_latent,
    query_rope,
    latent_cache,
    rope_cache,
    lengths,
    moe_input,
    routes,
    route_weight,
    gate_weight,
    up_weight,
    down_weight,
):
    attended = attend(query_latent, query_rope, latent_cache, rope_cache, lengths)
    feature_count = moe_input.shape[1]
    top = routes.shape[1]
    packed = jnp.concatenate(
        [moe_input, routes.astype(jnp.bfloat16), route_weight.astype(jnp.bfloat16)], axis=1
    )
    pool = lax.all_gather(packed, "dev", axis=0, tiled=True)
    pool_rows = pool[:, :feature_count]
    pool_routes = pool[:, feature_count : feature_count + top].astype(jnp.int32)
    pool_weights = pool[:, feature_count + top :]
    node_count = lax.axis_size("node")
    dev_count = lax.axis_size("dev")
    expert_half = lax.axis_index("dev") // (dev_count // E_NODE)
    pooled = pool_rows.shape[0]
    slot_count = pooled * pool_routes.shape[1] // (E_NODE * node_count)
    targets = jnp.arange(node_count, dtype=jnp.int32) * E_NODE + expert_half
    matches = pool_routes[:, :, None] == targets[None, None, :]
    chosen = jnp.sum(matches.astype(jnp.int32), axis=1)
    route_share = jnp.sum(
        jnp.where(matches, pool_weights[:, :, None].astype(jnp.float32), 0.0), axis=1
    )
    before = jnp.cumsum(chosen, axis=0) - chosen
    copies = 1
    per_copy = slot_count // copies
    slot_index = jnp.arange(slot_count, dtype=jnp.int32).reshape(1, copies, per_copy, 1)
    selection = (chosen.T[:, None, None, :] == 1) & (before.T[:, None, None, :] == slot_index)
    selector = selection.astype(jnp.bfloat16)
    weighted = (selection.astype(jnp.float32) * route_share.T[:, None, None, :]).astype(
        jnp.bfloat16
    )
    outgoing = jnp.einsum("ncsp,pd->cnsd", selector, pool_rows, preferred_element_type=jnp.float32)
    outgoing = outgoing.astype(jnp.bfloat16).reshape(copies * node_count, per_copy, feature_count)
    weighted, outgoing = (weighted, outgoing)
    arrived = lax.all_to_all(outgoing, "node", split_axis=0, concat_axis=0, tiled=True)
    peer_count, slot_total, width_total = arrived.shape
    flattened = arrived.reshape(peer_count * slot_total, width_total)
    produced = expert_slice(flattened, gate_weight, up_weight, down_weight)
    partial_value = produced.reshape(peer_count, slot_total, width_total)
    returned = lax.all_to_all(partial_value, "node", split_axis=0, concat_axis=0, tiled=True)
    returned = returned.reshape(copies, node_count, slot_count // copies, feature_count)
    pool_sum = jnp.einsum("ncsp,cnsd->pd", weighted, returned, preferred_element_type=jnp.float32)
    if dev_count > 8:
        combined = lax.psum_scatter(pool_sum, "dev", scatter_dimension=0, tiled=True)
        return (attended, combined.astype(jnp.bfloat16))
    own = lax.axis_index("dev")
    rows_per = pooled // dev_count
    combined = lax.dynamic_slice_in_dim(pool_sum, own * rows_per, rows_per, 0)
    for shift in range(1, dev_count):
        target = (own + shift) % dev_count
        outgoing_part = lax.dynamic_slice_in_dim(pool_sum, target * rows_per, rows_per, 0)
        combined = combined + lax.ppermute(
            outgoing_part, "dev", [(i, (i + shift) % dev_count) for i in range(dev_count)]
        )
    return (attended, combined.astype(jnp.bfloat16))


def solution(mesh):
    in_specs = (
        P(("grp", "node", "dev"), None, None),
        P(("grp", "node", "dev"), None),
        P(("grp", "node", "dev"), None, None),
        P(("grp", "node", "dev"), None, None),
        P(("grp", "node", "dev")),
        P(("grp", "node", "dev"), None),
        P(("grp", "node", "dev"), None),
        P(("grp", "node", "dev"), None),
        P(("node", "dev"), None, None),
        P(("node", "dev"), None, None),
        P(("node", "dev"), None, None),
    )
    out_specs = (P(("grp", "node", "dev"), None, None), P(("grp", "node", "dev"), None))
    return jax.shard_map(shards, mesh=mesh, in_specs=in_specs, out_specs=out_specs, check_vma=False)
```

```python
import math

import jax
import jax.numpy as jnp
from jax import lax
from jax.experimental import pallas as pl
from jax.experimental.pallas import tpu as pltpu
from jax.sharding import PartitionSpec as P

E_NODE = 2


score_scale = 1.0 / math.sqrt(192.0)


def attention_scores(query_latent, rope_query, latent_block, rope_block):
    latent_part = jnp.einsum(
        "rhc,rtc->rht", query_latent, latent_block, preferred_element_type=jnp.float32
    )
    rope_part = jnp.einsum(
        "rhk,rkt->rht", rope_query, rope_block, preferred_element_type=jnp.float32
    )
    return score_scale * (latent_part + rope_part)


def expert_slice(tokens, gate_block, up_block, down_block):
    peers, slots, feature_count = tokens.shape
    rows = peers * slots
    hidden_count = gate_block.shape[2]
    width = min(256, hidden_count)
    steps = hidden_count // width

    def kernel(x_ref, gate_ref, up_ref, down_ref, out_ref, x_all, acc_ref):
        step = pl.program_id(0)

        @pl.when(step == 0)
        def _():
            acc_ref[...] = jnp.zeros_like(acc_ref)
            for peer in range(peers):
                x_all[peer * slots : (peer + 1) * slots, :] = x_ref[peer].astype(jnp.float32)

        x = x_all[...].astype(jnp.bfloat16)
        gate_sum = jnp.dot(x, gate_ref[...], preferred_element_type=jnp.float32)
        up_sum = jnp.dot(x, up_ref[...], preferred_element_type=jnp.float32)
        hidden = (gate_sum / (1.0 + jnp.exp(-gate_sum)) * up_sum).astype(jnp.bfloat16)
        acc_ref[...] += jnp.dot(hidden, down_ref[...], preferred_element_type=jnp.float32)

        @pl.when(step == steps - 1)
        def _():
            for peer in range(peers):
                out_ref[peer] = acc_ref[peer * slots : (peer + 1) * slots, :].astype(out_ref.dtype)

    return pl.pallas_call(
        kernel,
        grid=(steps,),
        in_specs=[
            pl.BlockSpec((peers, slots, feature_count), lambda j: (0, 0, 0)),
            pl.BlockSpec((None, feature_count, width), lambda j: (0, 0, j)),
            pl.BlockSpec((None, feature_count, width), lambda j: (0, 0, j)),
            pl.BlockSpec((None, width, feature_count), lambda j: (0, j, 0)),
        ],
        out_specs=pl.BlockSpec((peers, slots, feature_count), lambda j: (0, 0, 0)),
        out_shape=jax.ShapeDtypeStruct((peers, slots, feature_count), jnp.bfloat16),
        scratch_shapes=[
            pltpu.VMEM((rows, feature_count), jnp.float32),
            pltpu.VMEM((rows, feature_count), jnp.float32),
        ],
        compiler_params=pltpu.CompilerParams(
            dimension_semantics=("arbitrary",), vmem_limit_bytes=100 * 1024 * 1024
        ),
    )(tokens, gate_block, up_block, down_block)


def normalize(scores, usable):
    masked = jnp.where(usable, scores, -jnp.inf)
    largest = jnp.max(masked, axis=-1, keepdims=True)
    powers = jnp.exp(masked - largest)
    return (powers / jnp.sum(powers, axis=-1, keepdims=True)).astype(jnp.bfloat16)


def attend(query_latent, query_rope, latent_cache, rope_cache, lengths):
    requests, head_count, latent = query_latent.shape
    context = latent_cache.shape[1]
    rope_query = query_rope.reshape(requests, head_count, -1)
    position = lax.broadcasted_iota(jnp.int32, (1, 1, context), 2)
    usable = position < lengths[:, None, None]
    block_width = min(128, context)
    blocks_live = (jnp.max(lengths) + block_width - 1) // block_width

    def score_block(counter, scores):
        block_start = counter * block_width
        latent_block = lax.dynamic_slice_in_dim(latent_cache, block_start, block_width, 1)
        rope_block = lax.dynamic_slice_in_dim(rope_cache, block_start, block_width, 2)
        block_scores = attention_scores(query_latent, rope_query, latent_block, rope_block)
        return lax.dynamic_update_slice_in_dim(scores, block_scores, block_start, 2)

    empty_scores = jnp.full((requests, head_count, context), -jnp.inf, jnp.float32)
    scores = lax.fori_loop(0, blocks_live, score_block, empty_scores)
    weights = normalize(scores, usable)

    def value_block(counter, accumulated):
        block_start = counter * block_width
        weight_block = lax.dynamic_slice_in_dim(weights, block_start, block_width, 2)
        latent_block = lax.dynamic_slice_in_dim(latent_cache, block_start, block_width, 1)
        return accumulated + jnp.einsum(
            "rht,rtc->rhc", weight_block, latent_block, preferred_element_type=jnp.float32
        )

    output = lax.fori_loop(
        0, blocks_live, value_block, jnp.zeros((requests, head_count, latent), jnp.float32)
    )
    return output.astype(jnp.bfloat16)


def shards(
    query_latent,
    query_rope,
    latent_cache,
    rope_cache,
    lengths,
    moe_input,
    routes,
    route_weight,
    gate_weight,
    up_weight,
    down_weight,
):
    attended = attend(query_latent, query_rope, latent_cache, rope_cache, lengths)
    feature_count = moe_input.shape[1]
    top = routes.shape[1]
    packed = jnp.concatenate(
        [moe_input, routes.astype(jnp.bfloat16), route_weight.astype(jnp.bfloat16)], axis=1
    )
    pool = lax.all_gather(packed, "dev", axis=0, tiled=True)
    pool_rows = pool[:, :feature_count]
    pool_routes = pool[:, feature_count : feature_count + top].astype(jnp.int32)
    pool_weights = pool[:, feature_count + top :]
    node_count = lax.axis_size("node")
    dev_count = lax.axis_size("dev")
    expert_half = lax.axis_index("dev") // (dev_count // E_NODE)
    pooled = pool_rows.shape[0]
    slot_count = pooled * pool_routes.shape[1] // (E_NODE * node_count)
    targets = jnp.arange(node_count, dtype=jnp.int32) * E_NODE + expert_half
    matches = pool_routes[:, :, None] == targets[None, None, :]
    chosen = jnp.sum(matches.astype(jnp.int32), axis=1)
    route_share = jnp.sum(
        jnp.where(matches, pool_weights[:, :, None].astype(jnp.float32), 0.0), axis=1
    )
    before = jnp.cumsum(chosen, axis=0) - chosen
    slot_index = jnp.arange(slot_count, dtype=jnp.int32).reshape(1, slot_count, 1)
    selection = (chosen.T[:, None, :] == 1) & (before.T[:, None, :] == slot_index)
    selection = selection.reshape(node_count * slot_count, pooled)
    selector = selection.astype(jnp.bfloat16)
    route_rows = jnp.repeat(route_share.T, slot_count, axis=0)
    weighted = (selection.astype(jnp.float32) * route_rows).astype(jnp.bfloat16)
    outgoing = jnp.dot(selector, pool_rows, preferred_element_type=jnp.float32)
    outgoing = outgoing.astype(jnp.bfloat16).reshape(node_count, slot_count, feature_count)
    arrived = lax.all_to_all(outgoing, "node", split_axis=0, concat_axis=0, tiled=True)
    produced = expert_slice(arrived, gate_weight, up_weight, down_weight)
    returned = lax.all_to_all(produced, "node", split_axis=0, concat_axis=0, tiled=True)
    returned = returned.reshape(node_count * slot_count, feature_count)
    pool_sum = jnp.einsum("qp,qd->pd", weighted, returned, preferred_element_type=jnp.float32)
    if dev_count > 8:
        combined = lax.psum_scatter(pool_sum, "dev", scatter_dimension=0, tiled=True)
        return (attended, combined.astype(jnp.bfloat16))
    own = lax.axis_index("dev")
    rows_per = pooled // dev_count
    combined = lax.dynamic_slice_in_dim(pool_sum, own * rows_per, rows_per, 0)
    for shift in range(1, dev_count):
        target = (own + shift) % dev_count
        outgoing_part = lax.dynamic_slice_in_dim(pool_sum, target * rows_per, rows_per, 0)
        combined = combined + lax.ppermute(
            outgoing_part, "dev", [(i, (i + shift) % dev_count) for i in range(dev_count)]
        )
    return (attended, combined.astype(jnp.bfloat16))


def solution(mesh):
    in_specs = (
        P(("grp", "node", "dev"), None, None),
        P(("grp", "node", "dev"), None),
        P(("grp", "node", "dev"), None, None),
        P(("grp", "node", "dev"), None, None),
        P(("grp", "node", "dev")),
        P(("grp", "node", "dev"), None),
        P(("grp", "node", "dev"), None),
        P(("grp", "node", "dev"), None),
        P(("node", "dev"), None, None),
        P(("node", "dev"), None, None),
        P(("node", "dev"), None, None),
    )
    out_specs = (P(("grp", "node", "dev"), None, None), P(("grp", "node", "dev"), None))
    return jax.shard_map(shards, mesh=mesh, in_specs=in_specs, out_specs=out_specs, check_vma=False)
```

```python
import math

import jax
import jax.numpy as jnp
from jax import lax
from jax.experimental import pallas as pl
from jax.experimental.pallas import tpu as pltpu
from jax.sharding import PartitionSpec as P

E_NODE = 2


score_scale = 1.0 / math.sqrt(192.0)


def attention_scores(query_latent, rope_query, latent_block, rope_block):
    latent_part = jnp.einsum(
        "rhc,rtc->rht", query_latent, latent_block, preferred_element_type=jnp.float32
    )
    rope_part = jnp.einsum(
        "rhk,rkt->rht", rope_query, rope_block, preferred_element_type=jnp.float32
    )
    return score_scale * (latent_part + rope_part)


def expert_slice(tokens, gate_block, up_block, down_block):
    peers, slots, feature_count = tokens.shape
    rows = peers * slots
    hidden_count = gate_block.shape[2]
    width = min(256, hidden_count)
    steps = hidden_count // width

    def kernel(x_ref, gate_ref, up_ref, down_ref, out_ref, x_all, acc_ref):
        step = pl.program_id(0)

        @pl.when(step == 0)
        def _():
            acc_ref[...] = jnp.zeros_like(acc_ref)
            for peer in range(peers):
                x_all[peer * slots : (peer + 1) * slots, :] = x_ref[peer].astype(jnp.float32)

        x = x_all[...].astype(jnp.bfloat16)
        gate_sum = jnp.dot(x, gate_ref[...], preferred_element_type=jnp.float32)
        up_sum = jnp.dot(x, up_ref[...], preferred_element_type=jnp.float32)
        hidden = (gate_sum / (1.0 + jnp.exp(-gate_sum)) * up_sum).astype(jnp.bfloat16)
        acc_ref[...] += jnp.dot(hidden, down_ref[...], preferred_element_type=jnp.float32)

        @pl.when(step == steps - 1)
        def _():
            for peer in range(peers):
                out_ref[peer] = acc_ref[peer * slots : (peer + 1) * slots, :].astype(out_ref.dtype)

    return pl.pallas_call(
        kernel,
        grid=(steps,),
        in_specs=[
            pl.BlockSpec((peers, slots, feature_count), lambda j: (0, 0, 0)),
            pl.BlockSpec((None, feature_count, width), lambda j: (0, 0, j)),
            pl.BlockSpec((None, feature_count, width), lambda j: (0, 0, j)),
            pl.BlockSpec((None, width, feature_count), lambda j: (0, j, 0)),
        ],
        out_specs=pl.BlockSpec((peers, slots, feature_count), lambda j: (0, 0, 0)),
        out_shape=jax.ShapeDtypeStruct((peers, slots, feature_count), jnp.bfloat16),
        scratch_shapes=[
            pltpu.VMEM((rows, feature_count), jnp.float32),
            pltpu.VMEM((rows, feature_count), jnp.float32),
        ],
        compiler_params=pltpu.CompilerParams(
            dimension_semantics=("arbitrary",), vmem_limit_bytes=100 * 1024 * 1024
        ),
    )(tokens, gate_block, up_block, down_block)


def normalize(scores, usable):
    masked = jnp.where(usable, scores, -jnp.inf)
    largest = jnp.max(masked, axis=-1, keepdims=True)
    powers = jnp.exp(masked - largest)
    return (powers / jnp.sum(powers, axis=-1, keepdims=True)).astype(jnp.bfloat16)


def attend(query_latent, query_rope, latent_cache, rope_cache, lengths):
    requests, head_count, latent = query_latent.shape
    context = latent_cache.shape[1]
    rope_query = query_rope.reshape(requests, head_count, -1)
    position = lax.broadcasted_iota(jnp.int32, (1, 1, context), 2)
    usable = position < lengths[:, None, None]
    block_width = min(128, context)
    blocks_live = (jnp.max(lengths) + block_width - 1) // block_width

    def score_block(counter, scores):
        block_start = counter * block_width
        latent_block = lax.dynamic_slice_in_dim(latent_cache, block_start, block_width, 1)
        rope_block = lax.dynamic_slice_in_dim(rope_cache, block_start, block_width, 2)
        block_scores = attention_scores(query_latent, rope_query, latent_block, rope_block)
        return lax.dynamic_update_slice_in_dim(scores, block_scores, block_start, 2)

    empty_scores = jnp.full((requests, head_count, context), -jnp.inf, jnp.float32)
    scores = lax.fori_loop(0, blocks_live, score_block, empty_scores)
    weights = normalize(scores, usable)

    def value_block(counter, accumulated):
        block_start = counter * block_width
        weight_block = lax.dynamic_slice_in_dim(weights, block_start, block_width, 2)
        latent_block = lax.dynamic_slice_in_dim(latent_cache, block_start, block_width, 1)
        return accumulated + jnp.einsum(
            "rht,rtc->rhc", weight_block, latent_block, preferred_element_type=jnp.float32
        )

    output = lax.fori_loop(
        0, blocks_live, value_block, jnp.zeros((requests, head_count, latent), jnp.float32)
    )
    return output.astype(jnp.bfloat16)


def shards(
    query_latent,
    query_rope,
    latent_cache,
    rope_cache,
    lengths,
    moe_input,
    routes,
    route_weight,
    gate_weight,
    up_weight,
    down_weight,
):
    attended = attend(query_latent, query_rope, latent_cache, rope_cache, lengths)
    feature_count = moe_input.shape[1]
    top = routes.shape[1]
    extra = 2 * top
    column = lax.broadcasted_iota(jnp.int32, (moe_input.shape[0], feature_count + extra), 1)
    wide_rows = jnp.pad(moe_input, ((0, 0), (0, extra)))
    wide_routes = jnp.pad(routes.astype(jnp.bfloat16), ((0, 0), (feature_count, top)))
    wide_weights = jnp.pad(route_weight.astype(jnp.bfloat16), ((0, 0), (feature_count + top, 0)))
    packed = jnp.where(
        column < feature_count,
        wide_rows,
        jnp.where(column < feature_count + top, wide_routes, wide_weights),
    )
    pool = lax.all_gather(packed, "dev", axis=0, tiled=True)
    pool_rows = pool[:, :feature_count]
    pool_routes = pool[:, feature_count : feature_count + top].astype(jnp.float32)
    pool_weights = pool[:, feature_count + top :]
    node_count = lax.axis_size("node")
    dev_count = lax.axis_size("dev")
    expert_half = lax.axis_index("dev") // (dev_count // E_NODE)
    pooled = pool_rows.shape[0]
    slot_count = pooled * pool_routes.shape[1] // (E_NODE * node_count)
    targets = (jnp.arange(node_count, dtype=jnp.int32) * E_NODE + expert_half).astype(jnp.float32)
    matches = pool_routes[:, :, None] == targets[None, None, :]
    chosen = jnp.sum(matches.astype(jnp.float32), axis=1)
    route_share = jnp.sum(
        jnp.where(matches, pool_weights[:, :, None].astype(jnp.float32), 0.0), axis=1
    )
    before = jnp.cumsum(chosen, axis=0) - chosen
    slot_index = jnp.arange(slot_count, dtype=jnp.float32).reshape(1, slot_count, 1)
    selection = (chosen.T[:, None, :] == 1) & (before.T[:, None, :] == slot_index)
    selection = selection.reshape(node_count * slot_count, pooled)
    selector = selection.astype(jnp.bfloat16)
    route_rows = jnp.repeat(route_share.T, slot_count, axis=0)
    weighted = (selection.astype(jnp.float32) * route_rows).astype(jnp.bfloat16)
    outgoing = jnp.dot(selector, pool_rows, preferred_element_type=jnp.float32)
    outgoing = outgoing.astype(jnp.bfloat16).reshape(node_count, slot_count, feature_count)
    arrived = lax.all_to_all(outgoing, "node", split_axis=0, concat_axis=0, tiled=True)
    produced = expert_slice(arrived, gate_weight, up_weight, down_weight)
    returned = lax.all_to_all(produced, "node", split_axis=0, concat_axis=0, tiled=True)
    returned = returned.reshape(node_count * slot_count, feature_count)
    pool_sum = jnp.einsum("qp,qd->pd", weighted, returned, preferred_element_type=jnp.float32)
    if dev_count > 8:
        combined = lax.psum_scatter(pool_sum, "dev", scatter_dimension=0, tiled=True)
        return (attended, combined.astype(jnp.bfloat16))
    own = lax.axis_index("dev")
    rows_per = pooled // dev_count
    combined = lax.dynamic_slice_in_dim(pool_sum, own * rows_per, rows_per, 0)
    for shift in range(1, dev_count):
        target = (own + shift) % dev_count
        outgoing_part = lax.dynamic_slice_in_dim(pool_sum, target * rows_per, rows_per, 0)
        combined = combined + lax.ppermute(
            outgoing_part, "dev", [(i, (i + shift) % dev_count) for i in range(dev_count)]
        )
    return (attended, combined.astype(jnp.bfloat16))


def solution(mesh):
    in_specs = (
        P(("grp", "node", "dev"), None, None),
        P(("grp", "node", "dev"), None),
        P(("grp", "node", "dev"), None, None),
        P(("grp", "node", "dev"), None, None),
        P(("grp", "node", "dev")),
        P(("grp", "node", "dev"), None),
        P(("grp", "node", "dev"), None),
        P(("grp", "node", "dev"), None),
        P(("node", "dev"), None, None),
        P(("node", "dev"), None, None),
        P(("node", "dev"), None, None),
    )
    out_specs = (P(("grp", "node", "dev"), None, None), P(("grp", "node", "dev"), None))
    return jax.shard_map(shards, mesh=mesh, in_specs=in_specs, out_specs=out_specs, check_vma=False)
```

```python
import math

import jax
import jax.numpy as jnp
from jax import lax
from jax.experimental import pallas as pl
from jax.experimental.pallas import tpu as pltpu
from jax.sharding import PartitionSpec as P

E_NODE = 2


score_scale = 1.0 / math.sqrt(192.0)


def attention_scores(query_latent, rope_query, latent_block, rope_block):
    latent_part = jnp.einsum(
        "rhc,rtc->rht", query_latent, latent_block, preferred_element_type=jnp.float32
    )
    rope_part = jnp.einsum(
        "rhk,rkt->rht", rope_query, rope_block, preferred_element_type=jnp.float32
    )
    return score_scale * (latent_part + rope_part)


def expert_slice(tokens, gate_block, up_block, down_block):
    peers, slots, feature_count = tokens.shape
    rows = peers * slots
    hidden_count = gate_block.shape[2]
    width = min(256, hidden_count)
    blocks = hidden_count // width

    def kernel(x_ref, gate_hbm, up_hbm, down_hbm, out_ref, gate_buf, up_buf, down_buf, sems, x_all, acc_ref):
        copies = []
        for block in range(blocks):
            window = pl.ds(block * width, width)
            gate_copy = pltpu.make_async_copy(gate_hbm.at[0, :, window], gate_buf.at[block], sems.at[0, block])
            up_copy = pltpu.make_async_copy(up_hbm.at[0, :, window], up_buf.at[block], sems.at[1, block])
            down_copy = pltpu.make_async_copy(down_hbm.at[0, window, :], down_buf.at[block], sems.at[2, block])
            gate_copy.start()
            up_copy.start()
            down_copy.start()
            copies.append((gate_copy, up_copy, down_copy))
        for peer in range(peers):
            x_all[peer * slots : (peer + 1) * slots, :] = x_ref[peer].astype(jnp.float32)
        x = x_all[...].astype(jnp.bfloat16)
        acc_ref[...] = jnp.zeros_like(acc_ref)
        for block in range(blocks):
            gate_copy, up_copy, down_copy = copies[block]
            gate_copy.wait()
            up_copy.wait()
            gate_sum = jnp.dot(x, gate_buf[block], preferred_element_type=jnp.float32)
            up_sum = jnp.dot(x, up_buf[block], preferred_element_type=jnp.float32)
            hidden = (gate_sum / (1.0 + jnp.exp(-gate_sum)) * up_sum).astype(jnp.bfloat16)
            down_copy.wait()
            acc_ref[...] += jnp.dot(hidden, down_buf[block], preferred_element_type=jnp.float32)
        for peer in range(peers):
            out_ref[peer] = acc_ref[peer * slots : (peer + 1) * slots, :].astype(out_ref.dtype)

    return pl.pallas_call(
        kernel,
        in_specs=[pl.BlockSpec(memory_space=pltpu.VMEM)] + [pl.BlockSpec(memory_space=pl.ANY)] * 3,
        out_specs=pl.BlockSpec(memory_space=pltpu.VMEM),
        out_shape=jax.ShapeDtypeStruct((peers, slots, feature_count), jnp.bfloat16),
        scratch_shapes=[
            pltpu.VMEM((blocks, feature_count, width), gate_block.dtype),
            pltpu.VMEM((blocks, feature_count, width), up_block.dtype),
            pltpu.VMEM((blocks, width, feature_count), down_block.dtype),
            pltpu.SemaphoreType.DMA((3, blocks)),
            pltpu.VMEM((rows, feature_count), jnp.float32),
            pltpu.VMEM((rows, feature_count), jnp.float32),
        ],
        compiler_params=pltpu.CompilerParams(vmem_limit_bytes=60 * 1024 * 1024),
    )(tokens, gate_block, up_block, down_block)


def normalize(scores, usable):
    masked = jnp.where(usable, scores, -jnp.inf)
    largest = jnp.max(masked, axis=-1, keepdims=True)
    powers = jnp.exp(masked - largest)
    return (powers / jnp.sum(powers, axis=-1, keepdims=True)).astype(jnp.bfloat16)


def attend(query_latent, query_rope, latent_cache, rope_cache, lengths):
    requests, head_count, latent = query_latent.shape
    context = latent_cache.shape[1]
    rope_query = query_rope.reshape(requests, head_count, -1)
    position = lax.broadcasted_iota(jnp.int32, (1, 1, context), 2)
    usable = position < lengths[:, None, None]
    block_width = min(128, context)
    blocks_live = (jnp.max(lengths) + block_width - 1) // block_width

    def score_block(counter, scores):
        block_start = counter * block_width
        latent_block = lax.dynamic_slice_in_dim(latent_cache, block_start, block_width, 1)
        rope_block = lax.dynamic_slice_in_dim(rope_cache, block_start, block_width, 2)
        block_scores = attention_scores(query_latent, rope_query, latent_block, rope_block)
        return lax.dynamic_update_slice_in_dim(scores, block_scores, block_start, 2)

    empty_scores = jnp.full((requests, head_count, context), -jnp.inf, jnp.float32)
    scores = lax.fori_loop(0, blocks_live, score_block, empty_scores)
    weights = normalize(scores, usable)

    def value_block(counter, accumulated):
        block_start = counter * block_width
        weight_block = lax.dynamic_slice_in_dim(weights, block_start, block_width, 2)
        latent_block = lax.dynamic_slice_in_dim(latent_cache, block_start, block_width, 1)
        return accumulated + jnp.einsum(
            "rht,rtc->rhc", weight_block, latent_block, preferred_element_type=jnp.float32
        )

    output = lax.fori_loop(
        0, blocks_live, value_block, jnp.zeros((requests, head_count, latent), jnp.float32)
    )
    return output.astype(jnp.bfloat16)


def shards(
    query_latent,
    query_rope,
    latent_cache,
    rope_cache,
    lengths,
    moe_input,
    routes,
    route_weight,
    gate_weight,
    up_weight,
    down_weight,
):
    attended = attend(query_latent, query_rope, latent_cache, rope_cache, lengths)
    feature_count = moe_input.shape[1]
    top = routes.shape[1]
    extra = 2 * top
    column = lax.broadcasted_iota(jnp.int32, (moe_input.shape[0], feature_count + extra), 1)
    wide_rows = jnp.pad(moe_input, ((0, 0), (0, extra)))
    wide_routes = jnp.pad(routes.astype(jnp.bfloat16), ((0, 0), (feature_count, top)))
    wide_weights = jnp.pad(route_weight.astype(jnp.bfloat16), ((0, 0), (feature_count + top, 0)))
    packed = jnp.where(
        column < feature_count,
        wide_rows,
        jnp.where(column < feature_count + top, wide_routes, wide_weights),
    )
    pool = lax.all_gather(packed, "dev", axis=0, tiled=True)
    pool_rows = pool[:, :feature_count]
    pool_routes = pool[:, feature_count : feature_count + top].astype(jnp.float32)
    pool_weights = pool[:, feature_count + top :]
    node_count = lax.axis_size("node")
    dev_count = lax.axis_size("dev")
    expert_half = lax.axis_index("dev") // (dev_count // E_NODE)
    pooled = pool_rows.shape[0]
    slot_count = pooled * pool_routes.shape[1] // (E_NODE * node_count)
    targets = (jnp.arange(node_count, dtype=jnp.int32) * E_NODE + expert_half).astype(jnp.float32)
    matches = pool_routes[:, :, None] == targets[None, None, :]
    chosen = jnp.sum(matches.astype(jnp.float32), axis=1)
    route_share = jnp.sum(
        jnp.where(matches, pool_weights[:, :, None].astype(jnp.float32), 0.0), axis=1
    )
    before = jnp.cumsum(chosen, axis=0) - chosen
    slot_index = jnp.arange(slot_count, dtype=jnp.float32).reshape(1, slot_count, 1)
    selection = (chosen.T[:, None, :] == 1) & (before.T[:, None, :] == slot_index)
    selection = selection.reshape(node_count * slot_count, pooled)
    selector = selection.astype(jnp.bfloat16)
    route_rows = jnp.repeat(route_share.T, slot_count, axis=0)
    weighted = (selection.astype(jnp.float32) * route_rows).astype(jnp.bfloat16)
    outgoing = jnp.dot(selector, pool_rows, preferred_element_type=jnp.float32)
    outgoing = outgoing.astype(jnp.bfloat16).reshape(node_count, slot_count, feature_count)
    arrived = lax.all_to_all(outgoing, "node", split_axis=0, concat_axis=0, tiled=True)
    produced = expert_slice(arrived, gate_weight, up_weight, down_weight)
    returned = lax.all_to_all(produced, "node", split_axis=0, concat_axis=0, tiled=True)
    returned = returned.reshape(node_count * slot_count, feature_count)
    pool_sum = jnp.einsum("qp,qd->pd", weighted, returned, preferred_element_type=jnp.float32)
    if dev_count > 8:
        combined = lax.psum_scatter(pool_sum, "dev", scatter_dimension=0, tiled=True)
        return (attended, combined.astype(jnp.bfloat16))
    own = lax.axis_index("dev")
    rows_per = pooled // dev_count
    combined = lax.dynamic_slice_in_dim(pool_sum, own * rows_per, rows_per, 0)
    for shift in range(1, dev_count):
        target = (own + shift) % dev_count
        outgoing_part = lax.dynamic_slice_in_dim(pool_sum, target * rows_per, rows_per, 0)
        combined = combined + lax.ppermute(
            outgoing_part, "dev", [(i, (i + shift) % dev_count) for i in range(dev_count)]
        )
    return (attended, combined.astype(jnp.bfloat16))


def solution(mesh):
    in_specs = (
        P(("grp", "node", "dev"), None, None),
        P(("grp", "node", "dev"), None),
        P(("grp", "node", "dev"), None, None),
        P(("grp", "node", "dev"), None, None),
        P(("grp", "node", "dev")),
        P(("grp", "node", "dev"), None),
        P(("grp", "node", "dev"), None),
        P(("grp", "node", "dev"), None),
        P(("node", "dev"), None, None),
        P(("node", "dev"), None, None),
        P(("node", "dev"), None, None),
    )
    out_specs = (P(("grp", "node", "dev"), None, None), P(("grp", "node", "dev"), None))
    return jax.shard_map(shards, mesh=mesh, in_specs=in_specs, out_specs=out_specs, check_vma=False)
```

```python
import math

import jax
import jax.numpy as jnp
from jax import lax
from jax.experimental import pallas as pl
from jax.experimental.pallas import tpu as pltpu
from jax.sharding import PartitionSpec as P

E_NODE = 2


score_scale = 1.0 / math.sqrt(192.0)


def attention_scores(query_latent, rope_query, latent_block, rope_block):
    latent_part = jnp.einsum(
        "rhc,rtc->rht", query_latent, latent_block, preferred_element_type=jnp.float32
    )
    rope_part = jnp.einsum(
        "rhk,rkt->rht", rope_query, rope_block, preferred_element_type=jnp.float32
    )
    return score_scale * (latent_part + rope_part)


def expert_slice(tokens, gate_block, up_block, down_block):
    peers, slots, feature_count = tokens.shape
    rows = peers * slots
    hidden_count = gate_block.shape[2]
    width = min(256, hidden_count)
    blocks = hidden_count // width

    def kernel(x_ref, gate_hbm, up_hbm, down_hbm, out_ref, gate_buf, up_buf, down_buf, sems, x_all, acc_ref):
        copies = []
        for block in range(blocks):
            window = pl.ds(block * width, width)
            gate_copy = pltpu.make_async_copy(gate_hbm.at[0, :, window], gate_buf.at[block], sems.at[0, block])
            up_copy = pltpu.make_async_copy(up_hbm.at[0, :, window], up_buf.at[block], sems.at[1, block])
            down_copy = pltpu.make_async_copy(down_hbm.at[0, window, :], down_buf.at[block], sems.at[2, block])
            gate_copy.start()
            up_copy.start()
            down_copy.start()
            copies.append((gate_copy, up_copy, down_copy))
        for peer in range(peers):
            x_all[peer * slots : (peer + 1) * slots, :] = x_ref[peer].astype(jnp.float32)
        x = x_all[...].astype(jnp.bfloat16)
        acc_ref[...] = jnp.zeros_like(acc_ref)
        for block in range(blocks):
            gate_copy, up_copy, down_copy = copies[block]
            gate_copy.wait()
            up_copy.wait()
            gate_sum = jnp.dot(x, gate_buf[block], preferred_element_type=jnp.float32)
            up_sum = jnp.dot(x, up_buf[block], preferred_element_type=jnp.float32)
            hidden = (gate_sum / (1.0 + jnp.exp(-gate_sum)) * up_sum).astype(jnp.bfloat16)
            down_copy.wait()
            acc_ref[...] += jnp.dot(hidden, down_buf[block], preferred_element_type=jnp.float32)
        for peer in range(peers):
            out_ref[peer] = acc_ref[peer * slots : (peer + 1) * slots, :].astype(out_ref.dtype)

    return pl.pallas_call(
        kernel,
        in_specs=[pl.BlockSpec(memory_space=pltpu.VMEM)] + [pl.BlockSpec(memory_space=pl.ANY)] * 3,
        out_specs=pl.BlockSpec(memory_space=pltpu.VMEM),
        out_shape=jax.ShapeDtypeStruct((peers, slots, feature_count), jnp.bfloat16),
        scratch_shapes=[
            pltpu.VMEM((blocks, feature_count, width), gate_block.dtype),
            pltpu.VMEM((blocks, feature_count, width), up_block.dtype),
            pltpu.VMEM((blocks, width, feature_count), down_block.dtype),
            pltpu.SemaphoreType.DMA((3, blocks)),
            pltpu.VMEM((rows, feature_count), jnp.float32),
            pltpu.VMEM((rows, feature_count), jnp.float32),
        ],
        compiler_params=pltpu.CompilerParams(vmem_limit_bytes=60 * 1024 * 1024),
    )(tokens, gate_block, up_block, down_block)


def normalize(scores, usable):
    masked = jnp.where(usable, scores, -jnp.inf)
    largest = jnp.max(masked, axis=-1, keepdims=True)
    powers = jnp.exp(masked - largest)
    return (powers / jnp.sum(powers, axis=-1, keepdims=True)).astype(jnp.bfloat16)


def attend(query_latent, query_rope, latent_cache, rope_cache, lengths):
    requests, head_count, latent = query_latent.shape
    context = latent_cache.shape[1]
    rope_query = query_rope.reshape(requests, head_count, -1)
    position = lax.broadcasted_iota(jnp.int32, (1, 1, context), 2)
    usable = position < lengths[:, None, None]
    block_width = min(128, context)
    blocks_live = (jnp.max(lengths) + block_width - 1) // block_width

    def score_block(counter, scores):
        block_start = counter * block_width
        latent_block = lax.dynamic_slice_in_dim(latent_cache, block_start, block_width, 1)
        rope_block = lax.dynamic_slice_in_dim(rope_cache, block_start, block_width, 2)
        block_scores = attention_scores(query_latent, rope_query, latent_block, rope_block)
        return lax.dynamic_update_slice_in_dim(scores, block_scores, block_start, 2)

    empty_scores = jnp.full((requests, head_count, context), -jnp.inf, jnp.float32)
    scores = lax.fori_loop(0, blocks_live, score_block, empty_scores)
    weights = normalize(scores, usable)

    def value_block(counter, accumulated):
        block_start = counter * block_width
        weight_block = lax.dynamic_slice_in_dim(weights, block_start, block_width, 2)
        latent_block = lax.dynamic_slice_in_dim(latent_cache, block_start, block_width, 1)
        return accumulated + jnp.einsum(
            "rht,rtc->rhc", weight_block, latent_block, preferred_element_type=jnp.float32
        )

    output = lax.fori_loop(
        0, blocks_live, value_block, jnp.zeros((requests, head_count, latent), jnp.float32)
    )
    return output.astype(jnp.bfloat16)


def shards(
    query_latent,
    query_rope,
    latent_cache,
    rope_cache,
    lengths,
    moe_input,
    routes,
    route_weight,
    gate_weight,
    up_weight,
    down_weight,
):
    attended = attend(query_latent, query_rope, latent_cache, rope_cache, lengths)
    feature_count = moe_input.shape[1]
    top = routes.shape[1]
    extra = 2 * top
    column = lax.broadcasted_iota(jnp.int32, (moe_input.shape[0], feature_count + extra), 1)
    wide_rows = jnp.pad(moe_input, ((0, 0), (0, extra)))
    wide_routes = jnp.pad(routes.astype(jnp.bfloat16), ((0, 0), (feature_count, top)))
    wide_weights = jnp.pad(route_weight.astype(jnp.bfloat16), ((0, 0), (feature_count + top, 0)))
    packed = jnp.where(
        column < feature_count,
        wide_rows,
        jnp.where(column < feature_count + top, wide_routes, wide_weights),
    )
    pool = lax.all_gather(packed, "dev", axis=0, tiled=True)
    pool_rows = pool[:, :feature_count]
    pool_routes = pool[:, feature_count : feature_count + top].astype(jnp.float32)
    pool_weights = pool[:, feature_count + top :]
    node_count = lax.axis_size("node")
    dev_count = lax.axis_size("dev")
    expert_half = lax.axis_index("dev") // (dev_count // E_NODE)
    pooled = pool_rows.shape[0]
    slot_count = pooled * pool_routes.shape[1] // (E_NODE * node_count)
    targets = (jnp.arange(node_count, dtype=jnp.int32) * E_NODE + expert_half).astype(jnp.float32)
    matches = pool_routes[:, :, None] == targets[None, None, :]
    chosen = jnp.sum(matches.astype(jnp.float32), axis=1)
    route_share = jnp.sum(
        jnp.where(matches, pool_weights[:, :, None].astype(jnp.float32), 0.0), axis=1
    )
    before = jnp.cumsum(chosen, axis=0) - chosen
    slot_index = jnp.arange(slot_count, dtype=jnp.float32).reshape(1, slot_count, 1)
    selection = (chosen.T[:, None, :] == 1) & (before.T[:, None, :] == slot_index)
    selection = selection.reshape(node_count * slot_count, pooled)
    selector = selection.astype(jnp.bfloat16)
    route_rows = jnp.repeat(route_share.T, slot_count, axis=0)
    weighted = (selection.astype(jnp.float32) * route_rows).astype(jnp.bfloat16)
    outgoing = jnp.dot(selector, pool_rows, preferred_element_type=jnp.float32)
    outgoing = outgoing.astype(jnp.bfloat16).reshape(node_count, slot_count, feature_count)
    arrived = lax.all_to_all(outgoing, "node", split_axis=0, concat_axis=0, tiled=True)
    produced = expert_slice(arrived, gate_weight, up_weight, down_weight)
    returned = lax.all_to_all(produced, "node", split_axis=0, concat_axis=0, tiled=True)
    returned = returned.reshape(node_count * slot_count, feature_count)
    pool_sum = jnp.einsum("qp,qd->pd", weighted, returned, preferred_element_type=jnp.float32)
    if dev_count > 8:
        combined = lax.psum_scatter(pool_sum, "dev", scatter_dimension=0, tiled=True)
        return (attended, combined.astype(jnp.bfloat16))
    own = lax.axis_index("dev")
    if dev_count == 4 and pooled == 4:
        pairs = pool_sum.reshape(2, 2, feature_count)
        core = own % 2
        keep = jnp.where(core == 0, pairs[:, 0], pairs[:, 1])
        send = jnp.where(core == 0, pairs[:, 1], pairs[:, 0])
        halves = keep + lax.ppermute(send, "dev", [(i, i ^ 1) for i in range(4)])
        chip = own // 2
        keep = jnp.where(chip == 0, halves[:1], halves[1:])
        send = jnp.where(chip == 0, halves[1:], halves[:1])
        combined = keep + lax.ppermute(send, "dev", [(i, i ^ 2) for i in range(4)])
        return (attended, combined.astype(jnp.bfloat16))
    rows_per = pooled // dev_count
    combined = lax.dynamic_slice_in_dim(pool_sum, own * rows_per, rows_per, 0)
    for shift in range(1, dev_count):
        target = (own + shift) % dev_count
        outgoing_part = lax.dynamic_slice_in_dim(pool_sum, target * rows_per, rows_per, 0)
        combined = combined + lax.ppermute(
            outgoing_part, "dev", [(i, (i + shift) % dev_count) for i in range(dev_count)]
        )
    return (attended, combined.astype(jnp.bfloat16))


def solution(mesh):
    in_specs = (
        P(("grp", "node", "dev"), None, None),
        P(("grp", "node", "dev"), None),
        P(("grp", "node", "dev"), None, None),
        P(("grp", "node", "dev"), None, None),
        P(("grp", "node", "dev")),
        P(("grp", "node", "dev"), None),
        P(("grp", "node", "dev"), None),
        P(("grp", "node", "dev"), None),
        P(("node", "dev"), None, None),
        P(("node", "dev"), None, None),
        P(("node", "dev"), None, None),
    )
    out_specs = (P(("grp", "node", "dev"), None, None), P(("grp", "node", "dev"), None))
    return jax.shard_map(shards, mesh=mesh, in_specs=in_specs, out_specs=out_specs, check_vma=False)
```

```python
import math

import jax
import jax.numpy as jnp
from jax import lax
from jax.experimental import pallas as pl
from jax.experimental.pallas import tpu as pltpu
from jax.sharding import PartitionSpec as P

E_NODE = 2


score_scale = 1.0 / math.sqrt(192.0)


def attention_scores(query_latent, rope_query, latent_block, rope_block):
    latent_part = jnp.einsum(
        "rhc,rtc->rht", query_latent, latent_block, preferred_element_type=jnp.float32
    )
    rope_part = jnp.einsum(
        "rhk,rkt->rht", rope_query, rope_block, preferred_element_type=jnp.float32
    )
    return score_scale * (latent_part + rope_part)


def expert_slice(tokens, gate_block, up_block, down_block):
    peers, slots, feature_count = tokens.shape
    rows = peers * slots
    hidden_count = gate_block.shape[2]
    width = min(256, hidden_count)
    blocks = hidden_count // width

    def kernel(x_ref, gate_hbm, up_hbm, down_hbm, out_ref, gate_buf, up_buf, down_buf, sems, x_all, acc_ref):
        copies = []
        for block in range(blocks):
            window = pl.ds(block * width, width)
            gate_copy = pltpu.make_async_copy(gate_hbm.at[0, :, window], gate_buf.at[block], sems.at[0, block])
            up_copy = pltpu.make_async_copy(up_hbm.at[0, :, window], up_buf.at[block], sems.at[1, block])
            down_copy = pltpu.make_async_copy(down_hbm.at[0, window, :], down_buf.at[block], sems.at[2, block])
            gate_copy.start()
            up_copy.start()
            down_copy.start()
            copies.append((gate_copy, up_copy, down_copy))
        for peer in range(peers):
            x_all[peer * slots : (peer + 1) * slots, :] = x_ref[peer].astype(jnp.float32)
        x = x_all[...].astype(jnp.bfloat16)
        acc_ref[...] = jnp.zeros_like(acc_ref)
        for block in range(blocks):
            gate_copy, up_copy, down_copy = copies[block]
            gate_copy.wait()
            up_copy.wait()
            gate_sum = jnp.dot(x, gate_buf[block], preferred_element_type=jnp.float32)
            up_sum = jnp.dot(x, up_buf[block], preferred_element_type=jnp.float32)
            hidden = (gate_sum / (1.0 + jnp.exp(-gate_sum)) * up_sum).astype(jnp.bfloat16)
            down_copy.wait()
            acc_ref[...] += jnp.dot(hidden, down_buf[block], preferred_element_type=jnp.float32)
        for peer in range(peers):
            out_ref[peer] = acc_ref[peer * slots : (peer + 1) * slots, :].astype(out_ref.dtype)

    return pl.pallas_call(
        kernel,
        in_specs=[pl.BlockSpec(memory_space=pltpu.VMEM)] + [pl.BlockSpec(memory_space=pl.ANY)] * 3,
        out_specs=pl.BlockSpec(memory_space=pltpu.VMEM),
        out_shape=jax.ShapeDtypeStruct((peers, slots, feature_count), jnp.bfloat16),
        scratch_shapes=[
            pltpu.VMEM((blocks, feature_count, width), gate_block.dtype),
            pltpu.VMEM((blocks, feature_count, width), up_block.dtype),
            pltpu.VMEM((blocks, width, feature_count), down_block.dtype),
            pltpu.SemaphoreType.DMA((3, blocks)),
            pltpu.VMEM((rows, feature_count), jnp.float32),
            pltpu.VMEM((rows, feature_count), jnp.float32),
        ],
        compiler_params=pltpu.CompilerParams(vmem_limit_bytes=60 * 1024 * 1024),
    )(pltpu.with_memory_space_constraint(tokens, pltpu.MemorySpace.VMEM), gate_block, up_block, down_block)


def normalize(scores, usable):
    masked = jnp.where(usable, scores, -jnp.inf)
    largest = jnp.max(masked, axis=-1, keepdims=True)
    powers = jnp.exp(masked - largest)
    return (powers / jnp.sum(powers, axis=-1, keepdims=True)).astype(jnp.bfloat16)


def attend(query_latent, query_rope, latent_cache, rope_cache, lengths):
    requests, head_count, latent = query_latent.shape
    context = latent_cache.shape[1]
    rope_query = query_rope.reshape(requests, head_count, -1)
    position = lax.broadcasted_iota(jnp.int32, (1, 1, context), 2)
    usable = position < lengths[:, None, None]
    block_width = min(128, context)
    blocks_live = (jnp.max(lengths) + block_width - 1) // block_width

    def score_block(counter, scores):
        block_start = counter * block_width
        latent_block = lax.dynamic_slice_in_dim(latent_cache, block_start, block_width, 1)
        rope_block = lax.dynamic_slice_in_dim(rope_cache, block_start, block_width, 2)
        block_scores = attention_scores(query_latent, rope_query, latent_block, rope_block)
        return lax.dynamic_update_slice_in_dim(scores, block_scores, block_start, 2)

    empty_scores = jnp.full((requests, head_count, context), -jnp.inf, jnp.float32)
    scores = lax.fori_loop(0, blocks_live, score_block, empty_scores)
    weights = normalize(scores, usable)

    def value_block(counter, accumulated):
        block_start = counter * block_width
        weight_block = lax.dynamic_slice_in_dim(weights, block_start, block_width, 2)
        latent_block = lax.dynamic_slice_in_dim(latent_cache, block_start, block_width, 1)
        return accumulated + jnp.einsum(
            "rht,rtc->rhc", weight_block, latent_block, preferred_element_type=jnp.float32
        )

    output = lax.fori_loop(
        0, blocks_live, value_block, jnp.zeros((requests, head_count, latent), jnp.float32)
    )
    return output.astype(jnp.bfloat16)


def shards(
    query_latent,
    query_rope,
    latent_cache,
    rope_cache,
    lengths,
    moe_input,
    routes,
    route_weight,
    gate_weight,
    up_weight,
    down_weight,
):
    attended = attend(query_latent, query_rope, latent_cache, rope_cache, lengths)
    feature_count = moe_input.shape[1]
    top = routes.shape[1]
    extra = 2 * top
    column = lax.broadcasted_iota(jnp.int32, (moe_input.shape[0], feature_count + extra), 1)
    wide_rows = jnp.pad(moe_input, ((0, 0), (0, extra)))
    wide_routes = jnp.pad(routes.astype(jnp.bfloat16), ((0, 0), (feature_count, top)))
    wide_weights = jnp.pad(route_weight.astype(jnp.bfloat16), ((0, 0), (feature_count + top, 0)))
    packed = jnp.where(
        column < feature_count,
        wide_rows,
        jnp.where(column < feature_count + top, wide_routes, wide_weights),
    )
    pool = lax.all_gather(packed, "dev", axis=0, tiled=True)
    pool_rows = pool[:, :feature_count]
    pool_routes = pool[:, feature_count : feature_count + top].astype(jnp.float32)
    pool_weights = pool[:, feature_count + top :]
    node_count = lax.axis_size("node")
    dev_count = lax.axis_size("dev")
    expert_half = lax.axis_index("dev") // (dev_count // E_NODE)
    pooled = pool_rows.shape[0]
    slot_count = pooled * pool_routes.shape[1] // (E_NODE * node_count)
    targets = (jnp.arange(node_count, dtype=jnp.int32) * E_NODE + expert_half).astype(jnp.float32)
    matches = pool_routes[:, :, None] == targets[None, None, :]
    chosen = jnp.sum(matches.astype(jnp.float32), axis=1)
    route_share = jnp.sum(
        jnp.where(matches, pool_weights[:, :, None].astype(jnp.float32), 0.0), axis=1
    )
    before = jnp.cumsum(chosen, axis=0) - chosen
    slot_index = jnp.arange(slot_count, dtype=jnp.float32).reshape(1, slot_count, 1)
    selection = (chosen.T[:, None, :] == 1) & (before.T[:, None, :] == slot_index)
    selection = selection.reshape(node_count * slot_count, pooled)
    selector = selection.astype(jnp.bfloat16)
    route_rows = jnp.repeat(route_share.T, slot_count, axis=0)
    weighted = (selection.astype(jnp.float32) * route_rows).astype(jnp.bfloat16)
    outgoing = jnp.dot(selector, pool_rows, preferred_element_type=jnp.float32)
    outgoing = outgoing.astype(jnp.bfloat16).reshape(node_count, slot_count, feature_count)
    arrived = lax.all_to_all(outgoing, "node", split_axis=0, concat_axis=0, tiled=True)
    produced = expert_slice(arrived, gate_weight, up_weight, down_weight)
    returned = lax.all_to_all(produced, "node", split_axis=0, concat_axis=0, tiled=True)
    returned = returned.reshape(node_count * slot_count, feature_count)
    pool_sum = jnp.einsum("qp,qd->pd", weighted, returned, preferred_element_type=jnp.float32)
    if dev_count > 8:
        combined = lax.psum_scatter(pool_sum, "dev", scatter_dimension=0, tiled=True)
        return (attended, combined.astype(jnp.bfloat16))
    own = lax.axis_index("dev")
    if dev_count == 4 and pooled == 4:
        pairs = pool_sum.reshape(2, 2, feature_count)
        core = own % 2
        keep = jnp.where(core == 0, pairs[:, 0], pairs[:, 1])
        send = jnp.where(core == 0, pairs[:, 1], pairs[:, 0])
        halves = keep + lax.ppermute(send, "dev", [(i, i ^ 1) for i in range(4)])
        chip = own // 2
        keep = jnp.where(chip == 0, halves[:1], halves[1:])
        send = jnp.where(chip == 0, halves[1:], halves[:1])
        combined = keep + lax.ppermute(send, "dev", [(i, i ^ 2) for i in range(4)])
        return (attended, combined.astype(jnp.bfloat16))
    rows_per = pooled // dev_count
    combined = lax.dynamic_slice_in_dim(pool_sum, own * rows_per, rows_per, 0)
    for shift in range(1, dev_count):
        target = (own + shift) % dev_count
        outgoing_part = lax.dynamic_slice_in_dim(pool_sum, target * rows_per, rows_per, 0)
        combined = combined + lax.ppermute(
            outgoing_part, "dev", [(i, (i + shift) % dev_count) for i in range(dev_count)]
        )
    return (attended, combined.astype(jnp.bfloat16))


def solution(mesh):
    in_specs = (
        P(("grp", "node", "dev"), None, None),
        P(("grp", "node", "dev"), None),
        P(("grp", "node", "dev"), None, None),
        P(("grp", "node", "dev"), None, None),
        P(("grp", "node", "dev")),
        P(("grp", "node", "dev"), None),
        P(("grp", "node", "dev"), None),
        P(("grp", "node", "dev"), None),
        P(("node", "dev"), None, None),
        P(("node", "dev"), None, None),
        P(("node", "dev"), None, None),
    )
    out_specs = (P(("grp", "node", "dev"), None, None), P(("grp", "node", "dev"), None))
    return jax.shard_map(shards, mesh=mesh, in_specs=in_specs, out_specs=out_specs, check_vma=False)
```

```python
import math

import jax
import jax.numpy as jnp
from jax import lax
from jax.experimental import pallas as pl
from jax.experimental.pallas import tpu as pltpu
from jax.sharding import PartitionSpec as P

E_NODE = 2


score_scale = 1.0 / math.sqrt(192.0)


def attention_scores(query_latent, rope_query, latent_block, rope_block):
    latent_part = jnp.einsum(
        "rhc,rtc->rht", query_latent, latent_block, preferred_element_type=jnp.float32
    )
    rope_part = jnp.einsum(
        "rhk,rkt->rht", rope_query, rope_block, preferred_element_type=jnp.float32
    )
    return score_scale * (latent_part + rope_part)


def expert_slice(token_parts, gate_block, up_block, down_block):
    peers, part_slots, feature_count = token_parts[0].shape
    part_count = len(token_parts)
    slots = part_slots * part_count
    rows = peers * slots
    hidden_count = gate_block.shape[2]
    width = min(256, hidden_count)
    blocks = hidden_count // width

    def kernel(*refs):
        x_refs = refs[:part_count]
        gate_hbm, up_hbm, down_hbm, out_ref, gate_buf, up_buf, down_buf, sems, x_all, acc_ref = refs[part_count:]
        copies = []
        for block in range(blocks):
            window = pl.ds(block * width, width)
            gate_copy = pltpu.make_async_copy(gate_hbm.at[0, :, window], gate_buf.at[block], sems.at[0, block])
            up_copy = pltpu.make_async_copy(up_hbm.at[0, :, window], up_buf.at[block], sems.at[1, block])
            down_copy = pltpu.make_async_copy(down_hbm.at[0, window, :], down_buf.at[block], sems.at[2, block])
            gate_copy.start()
            up_copy.start()
            down_copy.start()
            copies.append((gate_copy, up_copy, down_copy))
        for peer in range(peers):
            for part, x_ref in enumerate(x_refs):
                start = peer * slots + part * part_slots
                x_all[start : start + part_slots, :] = x_ref[peer].astype(jnp.float32)
        x = x_all[...].astype(jnp.bfloat16)
        acc_ref[...] = jnp.zeros_like(acc_ref)
        for block in range(blocks):
            gate_copy, up_copy, down_copy = copies[block]
            gate_copy.wait()
            up_copy.wait()
            gate_sum = jnp.dot(x, gate_buf[block], preferred_element_type=jnp.float32)
            up_sum = jnp.dot(x, up_buf[block], preferred_element_type=jnp.float32)
            hidden = (gate_sum / (1.0 + jnp.exp(-gate_sum)) * up_sum).astype(jnp.bfloat16)
            down_copy.wait()
            acc_ref[...] += jnp.dot(hidden, down_buf[block], preferred_element_type=jnp.float32)
        for peer in range(peers):
            out_ref[peer] = acc_ref[peer * slots : (peer + 1) * slots, :].astype(out_ref.dtype)

    return pl.pallas_call(
        kernel,
        in_specs=[pl.BlockSpec(memory_space=pltpu.VMEM)] * part_count
        + [pl.BlockSpec(memory_space=pl.ANY)] * 3,
        out_specs=pl.BlockSpec(memory_space=pltpu.VMEM),
        out_shape=jax.ShapeDtypeStruct((peers, slots, feature_count), jnp.bfloat16),
        scratch_shapes=[
            pltpu.VMEM((blocks, feature_count, width), gate_block.dtype),
            pltpu.VMEM((blocks, feature_count, width), up_block.dtype),
            pltpu.VMEM((blocks, width, feature_count), down_block.dtype),
            pltpu.SemaphoreType.DMA((3, blocks)),
            pltpu.VMEM((rows, feature_count), jnp.float32),
            pltpu.VMEM((rows, feature_count), jnp.float32),
        ],
        compiler_params=pltpu.CompilerParams(vmem_limit_bytes=60 * 1024 * 1024),
    )(
        *[pltpu.with_memory_space_constraint(part, pltpu.MemorySpace.VMEM) for part in token_parts],
        gate_block,
        up_block,
        down_block,
    )


def normalize(scores, usable):
    masked = jnp.where(usable, scores, -jnp.inf)
    largest = jnp.max(masked, axis=-1, keepdims=True)
    powers = jnp.exp(masked - largest)
    return (powers / jnp.sum(powers, axis=-1, keepdims=True)).astype(jnp.bfloat16)


def attend(query_latent, query_rope, latent_cache, rope_cache, lengths):
    requests, head_count, latent = query_latent.shape
    context = latent_cache.shape[1]
    rope_query = query_rope.reshape(requests, head_count, -1)
    position = lax.broadcasted_iota(jnp.int32, (1, 1, context), 2)
    usable = position < lengths[:, None, None]
    block_width = min(128, context)
    blocks_live = (jnp.max(lengths) + block_width - 1) // block_width

    def score_block(counter, scores):
        block_start = counter * block_width
        latent_block = lax.dynamic_slice_in_dim(latent_cache, block_start, block_width, 1)
        rope_block = lax.dynamic_slice_in_dim(rope_cache, block_start, block_width, 2)
        block_scores = attention_scores(query_latent, rope_query, latent_block, rope_block)
        return lax.dynamic_update_slice_in_dim(scores, block_scores, block_start, 2)

    empty_scores = jnp.full((requests, head_count, context), -jnp.inf, jnp.float32)
    scores = lax.fori_loop(0, blocks_live, score_block, empty_scores)
    weights = normalize(scores, usable)

    def value_block(counter, accumulated):
        block_start = counter * block_width
        weight_block = lax.dynamic_slice_in_dim(weights, block_start, block_width, 2)
        latent_block = lax.dynamic_slice_in_dim(latent_cache, block_start, block_width, 1)
        return accumulated + jnp.einsum(
            "rht,rtc->rhc", weight_block, latent_block, preferred_element_type=jnp.float32
        )

    output = lax.fori_loop(
        0, blocks_live, value_block, jnp.zeros((requests, head_count, latent), jnp.float32)
    )
    return output.astype(jnp.bfloat16)


def shards(
    query_latent,
    query_rope,
    latent_cache,
    rope_cache,
    lengths,
    moe_input,
    routes,
    route_weight,
    gate_weight,
    up_weight,
    down_weight,
):
    attended = attend(query_latent, query_rope, latent_cache, rope_cache, lengths)
    feature_count = moe_input.shape[1]
    top = routes.shape[1]
    extra = 2 * top
    column = lax.broadcasted_iota(jnp.int32, (moe_input.shape[0], feature_count + extra), 1)
    wide_rows = jnp.pad(moe_input, ((0, 0), (0, extra)))
    wide_routes = jnp.pad(routes.astype(jnp.bfloat16), ((0, 0), (feature_count, top)))
    wide_weights = jnp.pad(route_weight.astype(jnp.bfloat16), ((0, 0), (feature_count + top, 0)))
    packed = jnp.where(
        column < feature_count,
        wide_rows,
        jnp.where(column < feature_count + top, wide_routes, wide_weights),
    )
    pool = lax.all_gather(packed, "dev", axis=0, tiled=True)
    pool_rows = pool[:, :feature_count]
    pool_routes = pool[:, feature_count : feature_count + top].astype(jnp.float32)
    pool_weights = pool[:, feature_count + top :]
    node_count = lax.axis_size("node")
    dev_count = lax.axis_size("dev")
    expert_half = lax.axis_index("dev") // (dev_count // E_NODE)
    pooled = pool_rows.shape[0]
    slot_count = pooled * pool_routes.shape[1] // (E_NODE * node_count)
    targets = (jnp.arange(node_count, dtype=jnp.int32) * E_NODE + expert_half).astype(jnp.float32)
    matches = pool_routes[:, :, None] == targets[None, None, :]
    chosen = jnp.sum(matches.astype(jnp.float32), axis=1)
    route_share = jnp.sum(
        jnp.where(matches, pool_weights[:, :, None].astype(jnp.float32), 0.0), axis=1
    )
    before = jnp.cumsum(chosen, axis=0) - chosen
    slot_index = jnp.arange(slot_count, dtype=jnp.float32).reshape(1, slot_count, 1)
    selection = (chosen.T[:, None, :] == 1) & (before.T[:, None, :] == slot_index)
    selection = selection.reshape(node_count * slot_count, pooled)
    selector = selection.astype(jnp.bfloat16)
    route_rows = jnp.repeat(route_share.T, slot_count, axis=0)
    weighted = (selection.astype(jnp.float32) * route_rows).astype(jnp.bfloat16)
    outgoing = jnp.dot(selector, pool_rows, preferred_element_type=jnp.float32)
    outgoing = outgoing.astype(jnp.bfloat16).reshape(node_count, slot_count, feature_count)
    if dev_count == 4 and slot_count == 2:
        core = lax.axis_index("dev") % 2
        mine = jnp.where(core == 0, outgoing[:, :1], outgoing[:, 1:])
        landed = lax.all_to_all(mine, "node", split_axis=0, concat_axis=0, tiled=True)
        partner = lax.ppermute(landed, "dev", [(i, i ^ 1) for i in range(4)])
        first = jnp.where(core == 0, landed, partner)
        second = jnp.where(core == 0, partner, landed)
        produced = expert_slice([first, second], gate_weight, up_weight, down_weight)
    else:
        arrived = lax.all_to_all(outgoing, "node", split_axis=0, concat_axis=0, tiled=True)
        produced = expert_slice([arrived], gate_weight, up_weight, down_weight)
    returned = lax.all_to_all(produced, "node", split_axis=0, concat_axis=0, tiled=True)
    returned = returned.reshape(node_count * slot_count, feature_count)
    pool_sum = jnp.einsum("qp,qd->pd", weighted, returned, preferred_element_type=jnp.float32)
    if dev_count > 8:
        combined = lax.psum_scatter(pool_sum, "dev", scatter_dimension=0, tiled=True)
        return (attended, combined.astype(jnp.bfloat16))
    own = lax.axis_index("dev")
    if dev_count == 4 and pooled == 4:
        pairs = pool_sum.reshape(2, 2, feature_count)
        core = own % 2
        keep = jnp.where(core == 0, pairs[:, 0], pairs[:, 1])
        send = jnp.where(core == 0, pairs[:, 1], pairs[:, 0])
        halves = keep + lax.ppermute(send, "dev", [(i, i ^ 1) for i in range(4)])
        chip = own // 2
        keep = jnp.where(chip == 0, halves[:1], halves[1:])
        send = jnp.where(chip == 0, halves[1:], halves[:1])
        combined = keep + lax.ppermute(send, "dev", [(i, i ^ 2) for i in range(4)])
        return (attended, combined.astype(jnp.bfloat16))
    rows_per = pooled // dev_count
    combined = lax.dynamic_slice_in_dim(pool_sum, own * rows_per, rows_per, 0)
    for shift in range(1, dev_count):
        target = (own + shift) % dev_count
        outgoing_part = lax.dynamic_slice_in_dim(pool_sum, target * rows_per, rows_per, 0)
        combined = combined + lax.ppermute(
            outgoing_part, "dev", [(i, (i + shift) % dev_count) for i in range(dev_count)]
        )
    return (attended, combined.astype(jnp.bfloat16))


def solution(mesh):
    in_specs = (
        P(("grp", "node", "dev"), None, None),
        P(("grp", "node", "dev"), None),
        P(("grp", "node", "dev"), None, None),
        P(("grp", "node", "dev"), None, None),
        P(("grp", "node", "dev")),
        P(("grp", "node", "dev"), None),
        P(("grp", "node", "dev"), None),
        P(("grp", "node", "dev"), None),
        P(("node", "dev"), None, None),
        P(("node", "dev"), None, None),
        P(("node", "dev"), None, None),
    )
    out_specs = (P(("grp", "node", "dev"), None, None), P(("grp", "node", "dev"), None))
    return jax.shard_map(shards, mesh=mesh, in_specs=in_specs, out_specs=out_specs, check_vma=False)
```

```python
import math

import jax
import jax.numpy as jnp
from jax import lax
from jax.experimental import pallas as pl
from jax.experimental.pallas import tpu as pltpu
from jax.sharding import PartitionSpec as P

E_NODE = 2


score_scale = 1.0 / math.sqrt(192.0)


def attention_scores(query_latent, rope_query, latent_block, rope_block):
    latent_part = jnp.einsum(
        "rhc,rtc->rht", query_latent, latent_block, preferred_element_type=jnp.float32
    )
    rope_part = jnp.einsum(
        "rhk,rkt->rht", rope_query, rope_block, preferred_element_type=jnp.float32
    )
    return score_scale * (latent_part + rope_part)


def prefetch_down(down_block, anchor, rows):
    feature_count = down_block.shape[2]

    def kernel(down_hbm, anchor_ref, down_out, sem):
        del anchor_ref
        copy = pltpu.make_async_copy(down_hbm.at[0, pl.ds(0, rows), :], down_out, sem.at[0])
        copy.start()
        copy.wait()

    return pl.pallas_call(
        kernel,
        in_specs=[pl.BlockSpec(memory_space=pl.ANY)] * 2,
        out_specs=pl.BlockSpec(memory_space=pltpu.VMEM),
        out_shape=pltpu.VMEM((rows, feature_count), down_block.dtype),
        scratch_shapes=[pltpu.SemaphoreType.DMA((1,))],
    )(down_block, anchor)


def expert_slice(tokens, gate_block, up_block, down_block, anchor):
    peers, slots, feature_count = tokens.shape
    rows = peers * slots
    hidden_count = gate_block.shape[2]
    width = min(256, hidden_count)
    blocks = hidden_count // width
    early = width // 2 if width >= 256 else 0
    extra = [prefetch_down(down_block, anchor, early)] if early else []

    def kernel(x_ref, gate_hbm, up_hbm, down_hbm, *rest):
        if early:
            down_first, out_ref, gate_buf, up_buf, down_buf, sems, x_all, acc_ref = rest
        else:
            out_ref, gate_buf, up_buf, down_buf, sems, x_all, acc_ref = rest
        copies = []
        for block in range(blocks):
            window = pl.ds(block * width, width)
            gate_copy = pltpu.make_async_copy(gate_hbm.at[0, :, window], gate_buf.at[block], sems.at[0, block])
            up_copy = pltpu.make_async_copy(up_hbm.at[0, :, window], up_buf.at[block], sems.at[1, block])
            if early and block == 0:
                down_copy = pltpu.make_async_copy(
                    down_hbm.at[0, pl.ds(early, width - early), :],
                    down_buf.at[0, pl.ds(early, width - early), :],
                    sems.at[2, 0],
                )
            else:
                down_copy = pltpu.make_async_copy(down_hbm.at[0, window, :], down_buf.at[block], sems.at[2, block])
            gate_copy.start()
            up_copy.start()
            down_copy.start()
            copies.append((gate_copy, up_copy, down_copy))
        for peer in range(peers):
            x_all[peer * slots : (peer + 1) * slots, :] = x_ref[peer].astype(jnp.float32)
        x = x_all[...].astype(jnp.bfloat16)
        acc_ref[...] = jnp.zeros_like(acc_ref)
        for block in range(blocks):
            gate_copy, up_copy, down_copy = copies[block]
            gate_copy.wait()
            up_copy.wait()
            gate_sum = jnp.dot(x, gate_buf[block], preferred_element_type=jnp.float32)
            up_sum = jnp.dot(x, up_buf[block], preferred_element_type=jnp.float32)
            hidden = (gate_sum / (1.0 + jnp.exp(-gate_sum)) * up_sum).astype(jnp.bfloat16)
            down_copy.wait()
            if early and block == 0:
                acc_ref[...] += jnp.dot(hidden[:, :early], down_first[...], preferred_element_type=jnp.float32)
                acc_ref[...] += jnp.dot(
                    hidden[:, early:], down_buf[0, early:, :], preferred_element_type=jnp.float32
                )
            else:
                acc_ref[...] += jnp.dot(hidden, down_buf[block], preferred_element_type=jnp.float32)
        for peer in range(peers):
            out_ref[peer] = acc_ref[peer * slots : (peer + 1) * slots, :].astype(out_ref.dtype)

    return pl.pallas_call(
        kernel,
        in_specs=[pl.BlockSpec(memory_space=pltpu.VMEM)]
        + [pl.BlockSpec(memory_space=pl.ANY)] * 3
        + [pl.BlockSpec(memory_space=pltpu.VMEM)] * len(extra),
        out_specs=pl.BlockSpec(memory_space=pltpu.VMEM),
        out_shape=jax.ShapeDtypeStruct((peers, slots, feature_count), jnp.bfloat16),
        scratch_shapes=[
            pltpu.VMEM((blocks, feature_count, width), gate_block.dtype),
            pltpu.VMEM((blocks, feature_count, width), up_block.dtype),
            pltpu.VMEM((blocks, width, feature_count), down_block.dtype),
            pltpu.SemaphoreType.DMA((3, blocks)),
            pltpu.VMEM((rows, feature_count), jnp.float32),
            pltpu.VMEM((rows, feature_count), jnp.float32),
        ],
        compiler_params=pltpu.CompilerParams(vmem_limit_bytes=60 * 1024 * 1024),
    )(
        pltpu.with_memory_space_constraint(tokens, pltpu.MemorySpace.VMEM),
        gate_block,
        up_block,
        down_block,
        *[pltpu.with_memory_space_constraint(part, pltpu.MemorySpace.VMEM) for part in extra],
    )


def normalize(scores, usable):
    masked = jnp.where(usable, scores, -jnp.inf)
    largest = jnp.max(masked, axis=-1, keepdims=True)
    powers = jnp.exp(masked - largest)
    return (powers / jnp.sum(powers, axis=-1, keepdims=True)).astype(jnp.bfloat16)


def attend(query_latent, query_rope, latent_cache, rope_cache, lengths):
    requests, head_count, latent = query_latent.shape
    context = latent_cache.shape[1]
    rope_query = query_rope.reshape(requests, head_count, -1)
    position = lax.broadcasted_iota(jnp.int32, (1, 1, context), 2)
    usable = position < lengths[:, None, None]
    block_width = min(128, context)
    blocks_live = (jnp.max(lengths) + block_width - 1) // block_width

    def score_block(counter, scores):
        block_start = counter * block_width
        latent_block = lax.dynamic_slice_in_dim(latent_cache, block_start, block_width, 1)
        rope_block = lax.dynamic_slice_in_dim(rope_cache, block_start, block_width, 2)
        block_scores = attention_scores(query_latent, rope_query, latent_block, rope_block)
        return lax.dynamic_update_slice_in_dim(scores, block_scores, block_start, 2)

    empty_scores = jnp.full((requests, head_count, context), -jnp.inf, jnp.float32)
    scores = lax.fori_loop(0, blocks_live, score_block, empty_scores)
    weights = normalize(scores, usable)

    def value_block(counter, accumulated):
        block_start = counter * block_width
        weight_block = lax.dynamic_slice_in_dim(weights, block_start, block_width, 2)
        latent_block = lax.dynamic_slice_in_dim(latent_cache, block_start, block_width, 1)
        return accumulated + jnp.einsum(
            "rht,rtc->rhc", weight_block, latent_block, preferred_element_type=jnp.float32
        )

    output = lax.fori_loop(
        0, blocks_live, value_block, jnp.zeros((requests, head_count, latent), jnp.float32)
    )
    return output.astype(jnp.bfloat16)


def shards(
    query_latent,
    query_rope,
    latent_cache,
    rope_cache,
    lengths,
    moe_input,
    routes,
    route_weight,
    gate_weight,
    up_weight,
    down_weight,
):
    attended = attend(query_latent, query_rope, latent_cache, rope_cache, lengths)
    feature_count = moe_input.shape[1]
    top = routes.shape[1]
    extra = 2 * top
    column = lax.broadcasted_iota(jnp.int32, (moe_input.shape[0], feature_count + extra), 1)
    wide_rows = jnp.pad(moe_input, ((0, 0), (0, extra)))
    wide_routes = jnp.pad(routes.astype(jnp.bfloat16), ((0, 0), (feature_count, top)))
    wide_weights = jnp.pad(route_weight.astype(jnp.bfloat16), ((0, 0), (feature_count + top, 0)))
    packed = jnp.where(
        column < feature_count,
        wide_rows,
        jnp.where(column < feature_count + top, wide_routes, wide_weights),
    )
    pool = lax.all_gather(packed, "dev", axis=0, tiled=True)
    pool_rows = pool[:, :feature_count]
    pool_routes = pool[:, feature_count : feature_count + top].astype(jnp.float32)
    pool_weights = pool[:, feature_count + top :]
    node_count = lax.axis_size("node")
    dev_count = lax.axis_size("dev")
    expert_half = lax.axis_index("dev") // (dev_count // E_NODE)
    pooled = pool_rows.shape[0]
    slot_count = pooled * pool_routes.shape[1] // (E_NODE * node_count)
    targets = (jnp.arange(node_count, dtype=jnp.int32) * E_NODE + expert_half).astype(jnp.float32)
    matches = pool_routes[:, :, None] == targets[None, None, :]
    chosen = jnp.sum(matches.astype(jnp.float32), axis=1)
    route_share = jnp.sum(
        jnp.where(matches, pool_weights[:, :, None].astype(jnp.float32), 0.0), axis=1
    )
    before = jnp.cumsum(chosen, axis=0) - chosen
    slot_index = jnp.arange(slot_count, dtype=jnp.float32).reshape(1, slot_count, 1)
    selection = (chosen.T[:, None, :] == 1) & (before.T[:, None, :] == slot_index)
    selection = selection.reshape(node_count * slot_count, pooled)
    selector = selection.astype(jnp.bfloat16)
    route_rows = jnp.repeat(route_share.T, slot_count, axis=0)
    weighted = (selection.astype(jnp.float32) * route_rows).astype(jnp.bfloat16)
    outgoing = jnp.dot(selector, pool_rows, preferred_element_type=jnp.float32)
    outgoing = outgoing.astype(jnp.bfloat16).reshape(node_count, slot_count, feature_count)
    arrived = lax.all_to_all(outgoing, "node", split_axis=0, concat_axis=0, tiled=True)
    produced = expert_slice(arrived, gate_weight, up_weight, down_weight, outgoing)
    returned = lax.all_to_all(produced, "node", split_axis=0, concat_axis=0, tiled=True)
    returned = returned.reshape(node_count * slot_count, feature_count)
    pool_sum = jnp.einsum("qp,qd->pd", weighted, returned, preferred_element_type=jnp.float32)
    if dev_count > 8:
        combined = lax.psum_scatter(pool_sum, "dev", scatter_dimension=0, tiled=True)
        return (attended, combined.astype(jnp.bfloat16))
    own = lax.axis_index("dev")
    if dev_count == 4 and pooled == 4:
        pairs = pool_sum.reshape(2, 2, feature_count)
        core = own % 2
        keep = jnp.where(core == 0, pairs[:, 0], pairs[:, 1])
        send = jnp.where(core == 0, pairs[:, 1], pairs[:, 0])
        halves = keep + lax.ppermute(send, "dev", [(i, i ^ 1) for i in range(4)])
        chip = own // 2
        keep = jnp.where(chip == 0, halves[:1], halves[1:])
        send = jnp.where(chip == 0, halves[1:], halves[:1])
        combined = keep + lax.ppermute(send, "dev", [(i, i ^ 2) for i in range(4)])
        return (attended, combined.astype(jnp.bfloat16))
    rows_per = pooled // dev_count
    combined = lax.dynamic_slice_in_dim(pool_sum, own * rows_per, rows_per, 0)
    for shift in range(1, dev_count):
        target = (own + shift) % dev_count
        outgoing_part = lax.dynamic_slice_in_dim(pool_sum, target * rows_per, rows_per, 0)
        combined = combined + lax.ppermute(
            outgoing_part, "dev", [(i, (i + shift) % dev_count) for i in range(dev_count)]
        )
    return (attended, combined.astype(jnp.bfloat16))


def solution(mesh):
    in_specs = (
        P(("grp", "node", "dev"), None, None),
        P(("grp", "node", "dev"), None),
        P(("grp", "node", "dev"), None, None),
        P(("grp", "node", "dev"), None, None),
        P(("grp", "node", "dev")),
        P(("grp", "node", "dev"), None),
        P(("grp", "node", "dev"), None),
        P(("grp", "node", "dev"), None),
        P(("node", "dev"), None, None),
        P(("node", "dev"), None, None),
        P(("node", "dev"), None, None),
    )
    out_specs = (P(("grp", "node", "dev"), None, None), P(("grp", "node", "dev"), None))
    return jax.shard_map(shards, mesh=mesh, in_specs=in_specs, out_specs=out_specs, check_vma=False)
```

```python
import math

import jax
import jax.numpy as jnp
from jax import lax
from jax.experimental import pallas as pl
from jax.experimental.pallas import tpu as pltpu
from jax.sharding import PartitionSpec as P

E_NODE = 2


score_scale = 1.0 / math.sqrt(192.0)


def attention_scores(query_latent, rope_query, latent_block, rope_block):
    latent_part = jnp.einsum(
        "rhc,rtc->rht", query_latent, latent_block, preferred_element_type=jnp.float32
    )
    rope_part = jnp.einsum(
        "rhk,rkt->rht", rope_query, rope_block, preferred_element_type=jnp.float32
    )
    return score_scale * (latent_part + rope_part)


def gather_rows(pool_rows, selector, node_count, slot_count):
    pooled, feature_count = pool_rows.shape

    def kernel(rows_ref, sel_ref, out_ref):
        picks = sel_ref[...].astype(jnp.float32)
        picked = picks[:, 0:1] * rows_ref[0:1, :].astype(jnp.float32)
        for source in range(1, pooled):
            picked = picked + picks[:, source : source + 1] * rows_ref[source : source + 1, :].astype(
                jnp.float32
            )
        for node in range(node_count):
            out_ref[node] = picked[node * slot_count : (node + 1) * slot_count].astype(out_ref.dtype)

    return pl.pallas_call(
        kernel,
        in_specs=[pl.BlockSpec(memory_space=pltpu.VMEM)] * 2,
        out_specs=pl.BlockSpec(memory_space=pltpu.VMEM),
        out_shape=jax.ShapeDtypeStruct((node_count, slot_count, feature_count), pool_rows.dtype),
    )(pool_rows, selector)


def prefetch_down(down_block, anchor, rows):
    feature_count = down_block.shape[2]

    def kernel(down_hbm, anchor_ref, down_out, sem):
        del anchor_ref
        copy = pltpu.make_async_copy(down_hbm.at[0, pl.ds(0, rows), :], down_out, sem.at[0])
        copy.start()
        copy.wait()

    return pl.pallas_call(
        kernel,
        in_specs=[pl.BlockSpec(memory_space=pl.ANY)] * 2,
        out_specs=pl.BlockSpec(memory_space=pltpu.VMEM),
        out_shape=pltpu.VMEM((rows, feature_count), down_block.dtype),
        scratch_shapes=[pltpu.SemaphoreType.DMA((1,))],
    )(down_block, anchor)


def expert_slice(tokens, gate_block, up_block, down_block, anchor):
    peers, slots, feature_count = tokens.shape
    rows = peers * slots
    hidden_count = gate_block.shape[2]
    width = min(256, hidden_count)
    blocks = hidden_count // width
    early = width // 2 if width >= 256 else 0
    extra = [prefetch_down(down_block, anchor, early)] if early else []

    def kernel(x_ref, gate_hbm, up_hbm, down_hbm, *rest):
        if early:
            down_first, out_ref, gate_buf, up_buf, down_buf, sems, x_all, acc_ref = rest
        else:
            out_ref, gate_buf, up_buf, down_buf, sems, x_all, acc_ref = rest
        copies = []
        for block in range(blocks):
            window = pl.ds(block * width, width)
            gate_copy = pltpu.make_async_copy(gate_hbm.at[0, :, window], gate_buf.at[block], sems.at[0, block])
            up_copy = pltpu.make_async_copy(up_hbm.at[0, :, window], up_buf.at[block], sems.at[1, block])
            if early and block == 0:
                down_copy = pltpu.make_async_copy(
                    down_hbm.at[0, pl.ds(early, width - early), :],
                    down_buf.at[0, pl.ds(early, width - early), :],
                    sems.at[2, 0],
                )
            else:
                down_copy = pltpu.make_async_copy(down_hbm.at[0, window, :], down_buf.at[block], sems.at[2, block])
            gate_copy.start()
            up_copy.start()
            down_copy.start()
            copies.append((gate_copy, up_copy, down_copy))
        for peer in range(peers):
            x_all[peer * slots : (peer + 1) * slots, :] = x_ref[peer].astype(jnp.float32)
        x = x_all[...].astype(jnp.bfloat16)
        acc_ref[...] = jnp.zeros_like(acc_ref)
        for block in range(blocks):
            gate_copy, up_copy, down_copy = copies[block]
            gate_copy.wait()
            up_copy.wait()
            gate_sum = jnp.dot(x, gate_buf[block], preferred_element_type=jnp.float32)
            up_sum = jnp.dot(x, up_buf[block], preferred_element_type=jnp.float32)
            hidden = (gate_sum / (1.0 + jnp.exp(-gate_sum)) * up_sum).astype(jnp.bfloat16)
            down_copy.wait()
            if early and block == 0:
                acc_ref[...] += jnp.dot(hidden[:, :early], down_first[...], preferred_element_type=jnp.float32)
                acc_ref[...] += jnp.dot(
                    hidden[:, early:], down_buf[0, early:, :], preferred_element_type=jnp.float32
                )
            else:
                acc_ref[...] += jnp.dot(hidden, down_buf[block], preferred_element_type=jnp.float32)
        for peer in range(peers):
            out_ref[peer] = acc_ref[peer * slots : (peer + 1) * slots, :].astype(out_ref.dtype)

    return pl.pallas_call(
        kernel,
        in_specs=[pl.BlockSpec(memory_space=pltpu.VMEM)]
        + [pl.BlockSpec(memory_space=pl.ANY)] * 3
        + [pl.BlockSpec(memory_space=pltpu.VMEM)] * len(extra),
        out_specs=pl.BlockSpec(memory_space=pltpu.VMEM),
        out_shape=jax.ShapeDtypeStruct((peers, slots, feature_count), jnp.bfloat16),
        scratch_shapes=[
            pltpu.VMEM((blocks, feature_count, width), gate_block.dtype),
            pltpu.VMEM((blocks, feature_count, width), up_block.dtype),
            pltpu.VMEM((blocks, width, feature_count), down_block.dtype),
            pltpu.SemaphoreType.DMA((3, blocks)),
            pltpu.VMEM((rows, feature_count), jnp.float32),
            pltpu.VMEM((rows, feature_count), jnp.float32),
        ],
        compiler_params=pltpu.CompilerParams(vmem_limit_bytes=60 * 1024 * 1024),
    )(
        pltpu.with_memory_space_constraint(tokens, pltpu.MemorySpace.VMEM),
        gate_block,
        up_block,
        down_block,
        *[pltpu.with_memory_space_constraint(part, pltpu.MemorySpace.VMEM) for part in extra],
    )


def normalize(scores, usable):
    masked = jnp.where(usable, scores, -jnp.inf)
    largest = jnp.max(masked, axis=-1, keepdims=True)
    powers = jnp.exp(masked - largest)
    return (powers / jnp.sum(powers, axis=-1, keepdims=True)).astype(jnp.bfloat16)


def attend(query_latent, query_rope, latent_cache, rope_cache, lengths):
    requests, head_count, latent = query_latent.shape
    context = latent_cache.shape[1]
    rope_query = query_rope.reshape(requests, head_count, -1)
    position = lax.broadcasted_iota(jnp.int32, (1, 1, context), 2)
    usable = position < lengths[:, None, None]
    block_width = min(128, context)
    blocks_live = (jnp.max(lengths) + block_width - 1) // block_width

    def score_block(counter, scores):
        block_start = counter * block_width
        latent_block = lax.dynamic_slice_in_dim(latent_cache, block_start, block_width, 1)
        rope_block = lax.dynamic_slice_in_dim(rope_cache, block_start, block_width, 2)
        block_scores = attention_scores(query_latent, rope_query, latent_block, rope_block)
        return lax.dynamic_update_slice_in_dim(scores, block_scores, block_start, 2)

    empty_scores = jnp.full((requests, head_count, context), -jnp.inf, jnp.float32)
    scores = lax.fori_loop(0, blocks_live, score_block, empty_scores)
    weights = normalize(scores, usable)

    def value_block(counter, accumulated):
        block_start = counter * block_width
        weight_block = lax.dynamic_slice_in_dim(weights, block_start, block_width, 2)
        latent_block = lax.dynamic_slice_in_dim(latent_cache, block_start, block_width, 1)
        return accumulated + jnp.einsum(
            "rht,rtc->rhc", weight_block, latent_block, preferred_element_type=jnp.float32
        )

    output = lax.fori_loop(
        0, blocks_live, value_block, jnp.zeros((requests, head_count, latent), jnp.float32)
    )
    return output.astype(jnp.bfloat16)


def shards(
    query_latent,
    query_rope,
    latent_cache,
    rope_cache,
    lengths,
    moe_input,
    routes,
    route_weight,
    gate_weight,
    up_weight,
    down_weight,
):
    attended = attend(query_latent, query_rope, latent_cache, rope_cache, lengths)
    feature_count = moe_input.shape[1]
    top = routes.shape[1]
    extra = 2 * top
    column = lax.broadcasted_iota(jnp.int32, (moe_input.shape[0], feature_count + extra), 1)
    wide_rows = jnp.pad(moe_input, ((0, 0), (0, extra)))
    wide_routes = jnp.pad(routes.astype(jnp.bfloat16), ((0, 0), (feature_count, top)))
    wide_weights = jnp.pad(route_weight.astype(jnp.bfloat16), ((0, 0), (feature_count + top, 0)))
    packed = jnp.where(
        column < feature_count,
        wide_rows,
        jnp.where(column < feature_count + top, wide_routes, wide_weights),
    )
    pool = lax.all_gather(packed, "dev", axis=0, tiled=True)
    pool_rows = pool[:, :feature_count]
    pool_routes = pool[:, feature_count : feature_count + top].astype(jnp.float32)
    pool_weights = pool[:, feature_count + top :]
    node_count = lax.axis_size("node")
    dev_count = lax.axis_size("dev")
    expert_half = lax.axis_index("dev") // (dev_count // E_NODE)
    pooled = pool_rows.shape[0]
    slot_count = pooled * pool_routes.shape[1] // (E_NODE * node_count)
    targets = (jnp.arange(node_count, dtype=jnp.int32) * E_NODE + expert_half).astype(jnp.float32)
    matches = pool_routes[:, :, None] == targets[None, None, :]
    chosen = jnp.sum(matches.astype(jnp.float32), axis=1)
    route_share = jnp.sum(
        jnp.where(matches, pool_weights[:, :, None].astype(jnp.float32), 0.0), axis=1
    )
    before = jnp.cumsum(chosen, axis=0) - chosen
    slot_index = jnp.arange(slot_count, dtype=jnp.float32).reshape(1, slot_count, 1)
    selection = (chosen.T[:, None, :] == 1) & (before.T[:, None, :] == slot_index)
    selection = selection.reshape(node_count * slot_count, pooled)
    selector = selection.astype(jnp.bfloat16)
    route_rows = jnp.repeat(route_share.T, slot_count, axis=0)
    weighted = (selection.astype(jnp.float32) * route_rows).astype(jnp.bfloat16)
    if pooled * node_count <= 64:
        outgoing = gather_rows(pool_rows, selector, node_count, slot_count)
    else:
        outgoing = jnp.dot(selector, pool_rows, preferred_element_type=jnp.float32)
        outgoing = outgoing.astype(jnp.bfloat16).reshape(node_count, slot_count, feature_count)
    arrived = lax.all_to_all(outgoing, "node", split_axis=0, concat_axis=0, tiled=True)
    produced = expert_slice(arrived, gate_weight, up_weight, down_weight, outgoing)
    returned = lax.all_to_all(produced, "node", split_axis=0, concat_axis=0, tiled=True)
    returned = returned.reshape(node_count * slot_count, feature_count)
    pool_sum = jnp.einsum("qp,qd->pd", weighted, returned, preferred_element_type=jnp.float32)
    if dev_count > 8:
        combined = lax.psum_scatter(pool_sum, "dev", scatter_dimension=0, tiled=True)
        return (attended, combined.astype(jnp.bfloat16))
    own = lax.axis_index("dev")
    if dev_count == 4 and pooled == 4:
        pairs = pool_sum.reshape(2, 2, feature_count)
        core = own % 2
        keep = jnp.where(core == 0, pairs[:, 0], pairs[:, 1])
        send = jnp.where(core == 0, pairs[:, 1], pairs[:, 0])
        halves = keep + lax.ppermute(send, "dev", [(i, i ^ 1) for i in range(4)])
        chip = own // 2
        keep = jnp.where(chip == 0, halves[:1], halves[1:])
        send = jnp.where(chip == 0, halves[1:], halves[:1])
        combined = keep + lax.ppermute(send, "dev", [(i, i ^ 2) for i in range(4)])
        return (attended, combined.astype(jnp.bfloat16))
    rows_per = pooled // dev_count
    combined = lax.dynamic_slice_in_dim(pool_sum, own * rows_per, rows_per, 0)
    for shift in range(1, dev_count):
        target = (own + shift) % dev_count
        outgoing_part = lax.dynamic_slice_in_dim(pool_sum, target * rows_per, rows_per, 0)
        combined = combined + lax.ppermute(
            outgoing_part, "dev", [(i, (i + shift) % dev_count) for i in range(dev_count)]
        )
    return (attended, combined.astype(jnp.bfloat16))


def solution(mesh):
    in_specs = (
        P(("grp", "node", "dev"), None, None),
        P(("grp", "node", "dev"), None),
        P(("grp", "node", "dev"), None, None),
        P(("grp", "node", "dev"), None, None),
        P(("grp", "node", "dev")),
        P(("grp", "node", "dev"), None),
        P(("grp", "node", "dev"), None),
        P(("grp", "node", "dev"), None),
        P(("node", "dev"), None, None),
        P(("node", "dev"), None, None),
        P(("node", "dev"), None, None),
    )
    out_specs = (P(("grp", "node", "dev"), None, None), P(("grp", "node", "dev"), None))
    return jax.shard_map(shards, mesh=mesh, in_specs=in_specs, out_specs=out_specs, check_vma=False)
```

```python
import math

import jax
import jax.numpy as jnp
from jax import lax
from jax.experimental import pallas as pl
from jax.experimental.pallas import tpu as pltpu
from jax.sharding import PartitionSpec as P

E_NODE = 2


score_scale = 1.0 / math.sqrt(192.0)


def attention_scores(query_latent, rope_query, latent_block, rope_block):
    latent_part = jnp.einsum(
        "rhc,rtc->rht", query_latent, latent_block, preferred_element_type=jnp.float32
    )
    rope_part = jnp.einsum(
        "rhk,rkt->rht", rope_query, rope_block, preferred_element_type=jnp.float32
    )
    return score_scale * (latent_part + rope_part)


def prefetch_down(down_block, anchor, rows):
    feature_count = down_block.shape[2]

    def kernel(down_hbm, anchor_ref, down_out, sem):
        del anchor_ref
        copy = pltpu.make_async_copy(down_hbm.at[0, pl.ds(0, rows), :], down_out, sem.at[0])
        copy.start()
        copy.wait()

    return pl.pallas_call(
        kernel,
        in_specs=[pl.BlockSpec(memory_space=pl.ANY)] * 2,
        out_specs=pl.BlockSpec(memory_space=pltpu.VMEM),
        out_shape=pltpu.VMEM((rows, feature_count), down_block.dtype),
        scratch_shapes=[pltpu.SemaphoreType.DMA((1,))],
    )(down_block, anchor)


def expert_slice(tokens, gate_block, up_block, down_block, anchor):
    peers, slots, feature_count = tokens.shape
    rows = peers * slots
    hidden_count = gate_block.shape[2]
    width = min(256, hidden_count)
    blocks = hidden_count // width
    early = width // 2 if width >= 256 else 0
    extra = [prefetch_down(down_block, anchor, early)] if early else []

    def kernel(x_ref, gate_hbm, up_hbm, down_hbm, *rest):
        if early:
            down_first, out_ref, gate_buf, up_buf, down_buf, sems, x_all, acc_ref = rest
        else:
            out_ref, gate_buf, up_buf, down_buf, sems, x_all, acc_ref = rest
        gate_copies = []
        for block in range(blocks):
            window = pl.ds(block * width, width)
            gate_copy = pltpu.make_async_copy(gate_hbm.at[0, :, window], gate_buf.at[block], sems.at[0, block])
            up_copy = pltpu.make_async_copy(up_hbm.at[0, :, window], up_buf.at[block], sems.at[1, block])
            gate_copy.start()
            up_copy.start()
            gate_copies.append((gate_copy, up_copy))
        down_copies = []
        for block in range(blocks):
            window = pl.ds(block * width, width)
            if early and block == 0:
                down_copy = pltpu.make_async_copy(
                    down_hbm.at[0, pl.ds(early, width - early), :],
                    down_buf.at[0, pl.ds(early, width - early), :],
                    sems.at[2, 0],
                )
            else:
                down_copy = pltpu.make_async_copy(down_hbm.at[0, window, :], down_buf.at[block], sems.at[2, block])
            down_copy.start()
            down_copies.append(down_copy)
        for peer in range(peers):
            x_all[peer * slots : (peer + 1) * slots, :] = x_ref[peer].astype(jnp.float32)
        x = x_all[...].astype(jnp.bfloat16)
        acc_ref[...] = jnp.zeros_like(acc_ref)
        hiddens = []
        for block in range(blocks):
            gate_copy, up_copy = gate_copies[block]
            gate_copy.wait()
            up_copy.wait()
            gate_sum = jnp.dot(x, gate_buf[block], preferred_element_type=jnp.float32)
            up_sum = jnp.dot(x, up_buf[block], preferred_element_type=jnp.float32)
            hiddens.append((gate_sum / (1.0 + jnp.exp(-gate_sum)) * up_sum).astype(jnp.bfloat16))
        for block in range(blocks):
            hidden = hiddens[block]
            down_copies[block].wait()
            if early and block == 0:
                acc_ref[...] += jnp.dot(hidden[:, :early], down_first[...], preferred_element_type=jnp.float32)
                acc_ref[...] += jnp.dot(
                    hidden[:, early:], down_buf[0, early:, :], preferred_element_type=jnp.float32
                )
            else:
                acc_ref[...] += jnp.dot(hidden, down_buf[block], preferred_element_type=jnp.float32)
        for peer in range(peers):
            out_ref[peer] = acc_ref[peer * slots : (peer + 1) * slots, :].astype(out_ref.dtype)

    return pl.pallas_call(
        kernel,
        in_specs=[pl.BlockSpec(memory_space=pltpu.VMEM)]
        + [pl.BlockSpec(memory_space=pl.ANY)] * 3
        + [pl.BlockSpec(memory_space=pltpu.VMEM)] * len(extra),
        out_specs=pl.BlockSpec(memory_space=pltpu.VMEM),
        out_shape=jax.ShapeDtypeStruct((peers, slots, feature_count), jnp.bfloat16),
        scratch_shapes=[
            pltpu.VMEM((blocks, feature_count, width), gate_block.dtype),
            pltpu.VMEM((blocks, feature_count, width), up_block.dtype),
            pltpu.VMEM((blocks, width, feature_count), down_block.dtype),
            pltpu.SemaphoreType.DMA((3, blocks)),
            pltpu.VMEM((rows, feature_count), jnp.float32),
            pltpu.VMEM((rows, feature_count), jnp.float32),
        ],
        compiler_params=pltpu.CompilerParams(vmem_limit_bytes=60 * 1024 * 1024),
    )(
        pltpu.with_memory_space_constraint(tokens, pltpu.MemorySpace.VMEM),
        gate_block,
        up_block,
        down_block,
        *[pltpu.with_memory_space_constraint(part, pltpu.MemorySpace.VMEM) for part in extra],
    )


def normalize(scores, usable):
    masked = jnp.where(usable, scores, -jnp.inf)
    largest = jnp.max(masked, axis=-1, keepdims=True)
    powers = jnp.exp(masked - largest)
    return (powers / jnp.sum(powers, axis=-1, keepdims=True)).astype(jnp.bfloat16)


def attend(query_latent, query_rope, latent_cache, rope_cache, lengths):
    requests, head_count, latent = query_latent.shape
    context = latent_cache.shape[1]
    rope_query = query_rope.reshape(requests, head_count, -1)
    position = lax.broadcasted_iota(jnp.int32, (1, 1, context), 2)
    usable = position < lengths[:, None, None]
    block_width = min(128, context)
    blocks_live = (jnp.max(lengths) + block_width - 1) // block_width

    def score_block(counter, scores):
        block_start = counter * block_width
        latent_block = lax.dynamic_slice_in_dim(latent_cache, block_start, block_width, 1)
        rope_block = lax.dynamic_slice_in_dim(rope_cache, block_start, block_width, 2)
        block_scores = attention_scores(query_latent, rope_query, latent_block, rope_block)
        return lax.dynamic_update_slice_in_dim(scores, block_scores, block_start, 2)

    empty_scores = jnp.full((requests, head_count, context), -jnp.inf, jnp.float32)
    scores = lax.fori_loop(0, blocks_live, score_block, empty_scores)
    weights = normalize(scores, usable)

    def value_block(counter, accumulated):
        block_start = counter * block_width
        weight_block = lax.dynamic_slice_in_dim(weights, block_start, block_width, 2)
        latent_block = lax.dynamic_slice_in_dim(latent_cache, block_start, block_width, 1)
        return accumulated + jnp.einsum(
            "rht,rtc->rhc", weight_block, latent_block, preferred_element_type=jnp.float32
        )

    output = lax.fori_loop(
        0, blocks_live, value_block, jnp.zeros((requests, head_count, latent), jnp.float32)
    )
    return output.astype(jnp.bfloat16)


def shards(
    query_latent,
    query_rope,
    latent_cache,
    rope_cache,
    lengths,
    moe_input,
    routes,
    route_weight,
    gate_weight,
    up_weight,
    down_weight,
):
    attended = attend(query_latent, query_rope, latent_cache, rope_cache, lengths)
    feature_count = moe_input.shape[1]
    top = routes.shape[1]
    extra = 2 * top
    column = lax.broadcasted_iota(jnp.int32, (moe_input.shape[0], feature_count + extra), 1)
    wide_rows = jnp.pad(moe_input, ((0, 0), (0, extra)))
    wide_routes = jnp.pad(routes.astype(jnp.bfloat16), ((0, 0), (feature_count, top)))
    wide_weights = jnp.pad(route_weight.astype(jnp.bfloat16), ((0, 0), (feature_count + top, 0)))
    packed = jnp.where(
        column < feature_count,
        wide_rows,
        jnp.where(column < feature_count + top, wide_routes, wide_weights),
    )
    pool = lax.all_gather(packed, "dev", axis=0, tiled=True)
    pool_rows = pool[:, :feature_count]
    pool_routes = pool[:, feature_count : feature_count + top].astype(jnp.float32)
    pool_weights = pool[:, feature_count + top :]
    node_count = lax.axis_size("node")
    dev_count = lax.axis_size("dev")
    expert_half = lax.axis_index("dev") // (dev_count // E_NODE)
    pooled = pool_rows.shape[0]
    slot_count = pooled * pool_routes.shape[1] // (E_NODE * node_count)
    targets = (jnp.arange(node_count, dtype=jnp.int32) * E_NODE + expert_half).astype(jnp.float32)
    matches = pool_routes[:, :, None] == targets[None, None, :]
    chosen = jnp.sum(matches.astype(jnp.float32), axis=1)
    route_share = jnp.sum(
        jnp.where(matches, pool_weights[:, :, None].astype(jnp.float32), 0.0), axis=1
    )
    before = jnp.cumsum(chosen, axis=0) - chosen
    slot_index = jnp.arange(slot_count, dtype=jnp.float32).reshape(1, slot_count, 1)
    selection = (chosen.T[:, None, :] == 1) & (before.T[:, None, :] == slot_index)
    selection = selection.reshape(node_count * slot_count, pooled)
    selector = selection.astype(jnp.bfloat16)
    route_rows = jnp.repeat(route_share.T, slot_count, axis=0)
    weighted = (selection.astype(jnp.float32) * route_rows).astype(jnp.bfloat16)
    outgoing = jnp.dot(selector, pool_rows, preferred_element_type=jnp.float32)
    outgoing = outgoing.astype(jnp.bfloat16).reshape(node_count, slot_count, feature_count)
    arrived = lax.all_to_all(outgoing, "node", split_axis=0, concat_axis=0, tiled=True)
    produced = expert_slice(arrived, gate_weight, up_weight, down_weight, outgoing)
    returned = lax.all_to_all(produced, "node", split_axis=0, concat_axis=0, tiled=True)
    returned = returned.reshape(node_count * slot_count, feature_count)
    pool_sum = jnp.einsum("qp,qd->pd", weighted, returned, preferred_element_type=jnp.float32)
    if dev_count > 8:
        combined = lax.psum_scatter(pool_sum, "dev", scatter_dimension=0, tiled=True)
        return (attended, combined.astype(jnp.bfloat16))
    own = lax.axis_index("dev")
    if dev_count == 4 and pooled == 4:
        pairs = pool_sum.reshape(2, 2, feature_count)
        core = own % 2
        keep = jnp.where(core == 0, pairs[:, 0], pairs[:, 1])
        send = jnp.where(core == 0, pairs[:, 1], pairs[:, 0])
        halves = keep + lax.ppermute(send, "dev", [(i, i ^ 1) for i in range(4)])
        chip = own // 2
        keep = jnp.where(chip == 0, halves[:1], halves[1:])
        send = jnp.where(chip == 0, halves[1:], halves[:1])
        combined = keep + lax.ppermute(send, "dev", [(i, i ^ 2) for i in range(4)])
        return (attended, combined.astype(jnp.bfloat16))
    rows_per = pooled // dev_count
    combined = lax.dynamic_slice_in_dim(pool_sum, own * rows_per, rows_per, 0)
    for shift in range(1, dev_count):
        target = (own + shift) % dev_count
        outgoing_part = lax.dynamic_slice_in_dim(pool_sum, target * rows_per, rows_per, 0)
        combined = combined + lax.ppermute(
            outgoing_part, "dev", [(i, (i + shift) % dev_count) for i in range(dev_count)]
        )
    return (attended, combined.astype(jnp.bfloat16))


def solution(mesh):
    in_specs = (
        P(("grp", "node", "dev"), None, None),
        P(("grp", "node", "dev"), None),
        P(("grp", "node", "dev"), None, None),
        P(("grp", "node", "dev"), None, None),
        P(("grp", "node", "dev")),
        P(("grp", "node", "dev"), None),
        P(("grp", "node", "dev"), None),
        P(("grp", "node", "dev"), None),
        P(("node", "dev"), None, None),
        P(("node", "dev"), None, None),
        P(("node", "dev"), None, None),
    )
    out_specs = (P(("grp", "node", "dev"), None, None), P(("grp", "node", "dev"), None))
    return jax.shard_map(shards, mesh=mesh, in_specs=in_specs, out_specs=out_specs, check_vma=False)
```

```python
import math

import jax
import jax.numpy as jnp
from jax import lax
from jax.experimental import pallas as pl
from jax.experimental.pallas import tpu as pltpu
from jax.sharding import PartitionSpec as P

E_NODE = 2


score_scale = 1.0 / math.sqrt(192.0)


def attention_scores(query_latent, rope_query, latent_block, rope_block):
    latent_part = jnp.einsum(
        "rhc,rtc->rht", query_latent, latent_block, preferred_element_type=jnp.float32
    )
    rope_part = jnp.einsum(
        "rhk,rkt->rht", rope_query, rope_block, preferred_element_type=jnp.float32
    )
    return score_scale * (latent_part + rope_part)


def prefetch_down(down_block, anchor, rows):
    feature_count = down_block.shape[2]

    def kernel(down_hbm, anchor_ref, down_out, sem):
        del anchor_ref
        copy = pltpu.make_async_copy(down_hbm.at[0, pl.ds(0, rows), :], down_out, sem.at[0])
        copy.start()
        copy.wait()

    return pl.pallas_call(
        kernel,
        in_specs=[pl.BlockSpec(memory_space=pl.ANY)] * 2,
        out_specs=pl.BlockSpec(memory_space=pltpu.VMEM),
        out_shape=pltpu.VMEM((rows, feature_count), down_block.dtype),
        scratch_shapes=[pltpu.SemaphoreType.DMA((1,))],
    )(down_block, anchor)


def expert_slice(tokens, gate_block, up_block, down_block, anchor):
    peers, slots, feature_count = tokens.shape
    rows = peers * slots
    hidden_count = gate_block.shape[2]
    width = min(256, hidden_count)
    blocks = hidden_count // width
    early = width // 2 if width >= 256 else 0
    extra = [prefetch_down(down_block, anchor, early)] if early else []

    def kernel(x_ref, gate_hbm, up_hbm, down_hbm, *rest):
        if early:
            down_first, out_ref, gate_buf, up_buf, down_buf, sems, x_all, acc_ref = rest
        else:
            out_ref, gate_buf, up_buf, down_buf, sems, x_all, acc_ref = rest
        copies = []
        for block in range(blocks):
            window = pl.ds(block * width, width)
            gate_copy = pltpu.make_async_copy(gate_hbm.at[0, :, window], gate_buf.at[block], sems.at[0, block])
            up_copy = pltpu.make_async_copy(up_hbm.at[0, :, window], up_buf.at[block], sems.at[1, block])
            if early and block == 0:
                down_copy = pltpu.make_async_copy(
                    down_hbm.at[0, pl.ds(early, width - early), :],
                    down_buf.at[0, pl.ds(early, width - early), :],
                    sems.at[2, 0],
                )
            else:
                down_copy = pltpu.make_async_copy(down_hbm.at[0, window, :], down_buf.at[block], sems.at[2, block])
            gate_copy.start()
            up_copy.start()
            down_copy.start()
            copies.append((gate_copy, up_copy, down_copy))
        for peer in range(peers):
            x_all[peer * slots : (peer + 1) * slots, :] = x_ref[peer].astype(jnp.float32)
        x = x_all[...].astype(jnp.bfloat16)
        acc_ref[...] = jnp.zeros_like(acc_ref)
        for block in range(blocks):
            gate_copy, up_copy, down_copy = copies[block]
            gate_copy.wait()
            up_copy.wait()
            gate_sum = jnp.dot(x, gate_buf[block], preferred_element_type=jnp.float32)
            up_sum = jnp.dot(x, up_buf[block], preferred_element_type=jnp.float32)
            hidden = (gate_sum / (1.0 + jnp.exp(-gate_sum)) * up_sum).astype(jnp.bfloat16)
            down_copy.wait()
            if early and block == 0:
                acc_ref[...] += jnp.dot(hidden[:, :early], down_first[...], preferred_element_type=jnp.float32)
                acc_ref[...] += jnp.dot(
                    hidden[:, early:], down_buf[0, early:, :], preferred_element_type=jnp.float32
                )
            else:
                acc_ref[...] += jnp.dot(hidden, down_buf[block], preferred_element_type=jnp.float32)
        for peer in range(peers):
            out_ref[peer] = acc_ref[peer * slots : (peer + 1) * slots, :].astype(out_ref.dtype)

    return pl.pallas_call(
        kernel,
        in_specs=[pl.BlockSpec(memory_space=pltpu.VMEM)]
        + [pl.BlockSpec(memory_space=pl.ANY)] * 3
        + [pl.BlockSpec(memory_space=pltpu.VMEM)] * len(extra),
        out_specs=pl.BlockSpec(memory_space=pltpu.VMEM),
        out_shape=jax.ShapeDtypeStruct((peers, slots, feature_count), jnp.bfloat16),
        scratch_shapes=[
            pltpu.VMEM((blocks, feature_count, width), gate_block.dtype),
            pltpu.VMEM((blocks, feature_count, width), up_block.dtype),
            pltpu.VMEM((blocks, width, feature_count), down_block.dtype),
            pltpu.SemaphoreType.DMA((3, blocks)),
            pltpu.VMEM((rows, feature_count), jnp.float32),
            pltpu.VMEM((rows, feature_count), jnp.float32),
        ],
        compiler_params=pltpu.CompilerParams(vmem_limit_bytes=60 * 1024 * 1024),
    )(
        pltpu.with_memory_space_constraint(tokens, pltpu.MemorySpace.VMEM),
        gate_block,
        up_block,
        down_block,
        *[pltpu.with_memory_space_constraint(part, pltpu.MemorySpace.VMEM) for part in extra],
    )


def normalize(scores, usable):
    masked = jnp.where(usable, scores, -jnp.inf)
    largest = jnp.max(masked, axis=-1, keepdims=True)
    powers = jnp.exp(masked - largest)
    return (powers / jnp.sum(powers, axis=-1, keepdims=True)).astype(jnp.bfloat16)


def attend(query_latent, query_rope, latent_cache, rope_cache, lengths):
    requests, head_count, latent = query_latent.shape
    context = latent_cache.shape[1]
    rope_query = query_rope.reshape(requests, head_count, -1)
    position = lax.broadcasted_iota(jnp.int32, (1, 1, context), 2)
    usable = position < lengths[:, None, None]
    block_width = min(128, context)
    blocks_live = (jnp.max(lengths) + block_width - 1) // block_width

    def score_block(counter, scores):
        block_start = counter * block_width
        latent_block = lax.dynamic_slice_in_dim(latent_cache, block_start, block_width, 1)
        rope_block = lax.dynamic_slice_in_dim(rope_cache, block_start, block_width, 2)
        block_scores = attention_scores(query_latent, rope_query, latent_block, rope_block)
        return lax.dynamic_update_slice_in_dim(scores, block_scores, block_start, 2)

    empty_scores = jnp.full((requests, head_count, context), -jnp.inf, jnp.float32)
    scores = lax.fori_loop(0, blocks_live, score_block, empty_scores)
    weights = normalize(scores, usable)

    def value_block(counter, accumulated):
        block_start = counter * block_width
        weight_block = lax.dynamic_slice_in_dim(weights, block_start, block_width, 2)
        latent_block = lax.dynamic_slice_in_dim(latent_cache, block_start, block_width, 1)
        return accumulated + jnp.einsum(
            "rht,rtc->rhc", weight_block, latent_block, preferred_element_type=jnp.float32
        )

    output = lax.fori_loop(
        0, blocks_live, value_block, jnp.zeros((requests, head_count, latent), jnp.float32)
    )
    return output.astype(jnp.bfloat16)


def shards(
    query_latent,
    query_rope,
    latent_cache,
    rope_cache,
    lengths,
    moe_input,
    routes,
    route_weight,
    gate_weight,
    up_weight,
    down_weight,
):
    attended = attend(query_latent, query_rope, latent_cache, rope_cache, lengths)
    feature_count = moe_input.shape[1]
    top = routes.shape[1]
    extra = 2 * top
    column = lax.broadcasted_iota(jnp.int32, (moe_input.shape[0], feature_count + extra), 1)
    wide_rows = jnp.pad(moe_input, ((0, 0), (0, extra)))
    wide_routes = jnp.pad(routes.astype(jnp.bfloat16), ((0, 0), (feature_count, top)))
    wide_weights = jnp.pad(route_weight.astype(jnp.bfloat16), ((0, 0), (feature_count + top, 0)))
    packed = jnp.where(
        column < feature_count,
        wide_rows,
        jnp.where(column < feature_count + top, wide_routes, wide_weights),
    )
    pool = lax.all_gather(packed, "dev", axis=0, tiled=True)
    pool_rows = pool[:, :feature_count]
    pool_routes = pool[:, feature_count : feature_count + top].astype(jnp.float32)
    pool_weights = pool[:, feature_count + top :]
    node_count = lax.axis_size("node")
    dev_count = lax.axis_size("dev")
    expert_half = lax.axis_index("dev") // (dev_count // E_NODE)
    pooled = pool_rows.shape[0]
    slot_count = pooled * pool_routes.shape[1] // (E_NODE * node_count)
    targets = (jnp.arange(node_count, dtype=jnp.int32) * E_NODE + expert_half).astype(jnp.float32)
    matches = pool_routes[:, :, None] == targets[None, None, :]
    chosen = jnp.sum(matches.astype(jnp.float32), axis=1)
    route_share = jnp.sum(
        jnp.where(matches, pool_weights[:, :, None].astype(jnp.float32), 0.0), axis=1
    )
    before = jnp.cumsum(chosen, axis=0) - chosen
    slot_index = jnp.arange(slot_count, dtype=jnp.float32).reshape(1, slot_count, 1)
    selection = (chosen.T[:, None, :] == 1) & (before.T[:, None, :] == slot_index)
    selection = selection.reshape(node_count * slot_count, pooled)
    selector = selection.astype(jnp.bfloat16)
    route_rows = jnp.repeat(route_share.T, slot_count, axis=0)
    weighted = (selection.astype(jnp.float32) * route_rows).astype(jnp.bfloat16)
    batched = selector.reshape(node_count, slot_count, pooled)
    outgoing = jnp.einsum(
        "nsp,npd->nsd",
        batched,
        jnp.broadcast_to(pool_rows[None], (node_count, pooled, feature_count)),
        preferred_element_type=jnp.float32,
    ).astype(jnp.bfloat16)
    arrived = lax.all_to_all(outgoing, "node", split_axis=0, concat_axis=0, tiled=True)
    produced = expert_slice(arrived, gate_weight, up_weight, down_weight, outgoing)
    returned = lax.all_to_all(produced, "node", split_axis=0, concat_axis=0, tiled=True)
    returned = returned.reshape(node_count * slot_count, feature_count)
    pool_sum = jnp.einsum("qp,qd->pd", weighted, returned, preferred_element_type=jnp.float32)
    if dev_count > 8:
        combined = lax.psum_scatter(pool_sum, "dev", scatter_dimension=0, tiled=True)
        return (attended, combined.astype(jnp.bfloat16))
    own = lax.axis_index("dev")
    if dev_count == 4 and pooled == 4:
        pairs = pool_sum.reshape(2, 2, feature_count)
        core = own % 2
        keep = jnp.where(core == 0, pairs[:, 0], pairs[:, 1])
        send = jnp.where(core == 0, pairs[:, 1], pairs[:, 0])
        halves = keep + lax.ppermute(send, "dev", [(i, i ^ 1) for i in range(4)])
        chip = own // 2
        keep = jnp.where(chip == 0, halves[:1], halves[1:])
        send = jnp.where(chip == 0, halves[1:], halves[:1])
        combined = keep + lax.ppermute(send, "dev", [(i, i ^ 2) for i in range(4)])
        return (attended, combined.astype(jnp.bfloat16))
    rows_per = pooled // dev_count
    combined = lax.dynamic_slice_in_dim(pool_sum, own * rows_per, rows_per, 0)
    for shift in range(1, dev_count):
        target = (own + shift) % dev_count
        outgoing_part = lax.dynamic_slice_in_dim(pool_sum, target * rows_per, rows_per, 0)
        combined = combined + lax.ppermute(
            outgoing_part, "dev", [(i, (i + shift) % dev_count) for i in range(dev_count)]
        )
    return (attended, combined.astype(jnp.bfloat16))


def solution(mesh):
    in_specs = (
        P(("grp", "node", "dev"), None, None),
        P(("grp", "node", "dev"), None),
        P(("grp", "node", "dev"), None, None),
        P(("grp", "node", "dev"), None, None),
        P(("grp", "node", "dev")),
        P(("grp", "node", "dev"), None),
        P(("grp", "node", "dev"), None),
        P(("grp", "node", "dev"), None),
        P(("node", "dev"), None, None),
        P(("node", "dev"), None, None),
        P(("node", "dev"), None, None),
    )
    out_specs = (P(("grp", "node", "dev"), None, None), P(("grp", "node", "dev"), None))
    return jax.shard_map(shards, mesh=mesh, in_specs=in_specs, out_specs=out_specs, check_vma=False)
```

```python
import math

import jax
import jax.numpy as jnp
from jax import lax
from jax.experimental import pallas as pl
from jax.experimental.pallas import tpu as pltpu
from jax.sharding import PartitionSpec as P

E_NODE = 2


score_scale = 1.0 / math.sqrt(192.0)


def attention_scores(query_latent, rope_query, latent_block, rope_block):
    latent_part = jnp.einsum(
        "rhc,rtc->rht", query_latent, latent_block, preferred_element_type=jnp.float32
    )
    rope_part = jnp.einsum(
        "rhk,rkt->rht", rope_query, rope_block, preferred_element_type=jnp.float32
    )
    return score_scale * (latent_part + rope_part)


def prefetch_down(down_block, anchor, rows):
    feature_count = down_block.shape[2]

    def kernel(down_hbm, anchor_ref, down_out, sem):
        del anchor_ref
        copy = pltpu.make_async_copy(down_hbm.at[0, pl.ds(0, rows), :], down_out, sem.at[0])
        copy.start()
        copy.wait()

    return pl.pallas_call(
        kernel,
        in_specs=[pl.BlockSpec(memory_space=pl.ANY)] * 2,
        out_specs=pl.BlockSpec(memory_space=pltpu.VMEM),
        out_shape=pltpu.VMEM((rows, feature_count), down_block.dtype),
        scratch_shapes=[pltpu.SemaphoreType.DMA((1,))],
    )(down_block, anchor)


def expert_slice(tokens, gate_block, up_block, down_block, anchor):
    peers, slots, feature_count = tokens.shape
    rows = peers * slots
    hidden_count = gate_block.shape[2]
    width = min(256, hidden_count)
    blocks = hidden_count // width
    early = width // 2 if width >= 256 else 0
    extra = [prefetch_down(down_block, anchor, early)] if early else []

    def kernel(x_ref, gate_hbm, up_hbm, down_hbm, *rest):
        if early:
            down_first, out_ref, gate_buf, up_buf, down_buf, sems, x_all, acc_ref = rest
        else:
            out_ref, gate_buf, up_buf, down_buf, sems, x_all, acc_ref = rest
        gate_copies = []
        for block in range(blocks):
            window = pl.ds(block * width, width)
            gate_copy = pltpu.make_async_copy(gate_hbm.at[0, :, window], gate_buf.at[block], sems.at[0, block])
            up_copy = pltpu.make_async_copy(up_hbm.at[0, :, window], up_buf.at[block], sems.at[1, block])
            gate_copy.start()
            up_copy.start()
            gate_copies.append((gate_copy, up_copy))
        down_copies = []
        for block in range(blocks):
            window = pl.ds(block * width, width)
            if early and block == 0:
                down_copy = pltpu.make_async_copy(
                    down_hbm.at[0, pl.ds(early, width - early), :],
                    down_buf.at[0, pl.ds(early, width - early), :],
                    sems.at[2, 0],
                )
            else:
                down_copy = pltpu.make_async_copy(down_hbm.at[0, window, :], down_buf.at[block], sems.at[2, block])
            down_copy.start()
            down_copies.append(down_copy)
        for peer in range(peers):
            x_all[peer * slots : (peer + 1) * slots, :] = x_ref[peer].astype(jnp.float32)
        x = x_all[...].astype(jnp.bfloat16)
        acc_ref[...] = jnp.zeros_like(acc_ref)
        hiddens = []
        for block in range(blocks):
            gate_copy, up_copy = gate_copies[block]
            gate_copy.wait()
            up_copy.wait()
            gate_sum = jnp.dot(x, gate_buf[block], preferred_element_type=jnp.float32)
            up_sum = jnp.dot(x, up_buf[block], preferred_element_type=jnp.float32)
            hiddens.append((gate_sum / (1.0 + jnp.exp(-gate_sum)) * up_sum).astype(jnp.bfloat16))
        for block in range(blocks):
            hidden = hiddens[block]
            down_copies[block].wait()
            if early and block == 0:
                acc_ref[...] += jnp.dot(hidden[:, :early], down_first[...], preferred_element_type=jnp.float32)
                acc_ref[...] += jnp.dot(
                    hidden[:, early:], down_buf[0, early:, :], preferred_element_type=jnp.float32
                )
            else:
                acc_ref[...] += jnp.dot(hidden, down_buf[block], preferred_element_type=jnp.float32)
        for peer in range(peers):
            out_ref[peer] = acc_ref[peer * slots : (peer + 1) * slots, :].astype(out_ref.dtype)

    return pl.pallas_call(
        kernel,
        in_specs=[pl.BlockSpec(memory_space=pltpu.VMEM)]
        + [pl.BlockSpec(memory_space=pl.ANY)] * 3
        + [pl.BlockSpec(memory_space=pltpu.VMEM)] * len(extra),
        out_specs=pl.BlockSpec(memory_space=pltpu.VMEM),
        out_shape=jax.ShapeDtypeStruct((peers, slots, feature_count), jnp.bfloat16),
        scratch_shapes=[
            pltpu.VMEM((blocks, feature_count, width), gate_block.dtype),
            pltpu.VMEM((blocks, feature_count, width), up_block.dtype),
            pltpu.VMEM((blocks, width, feature_count), down_block.dtype),
            pltpu.SemaphoreType.DMA((3, blocks)),
            pltpu.VMEM((rows, feature_count), jnp.float32),
            pltpu.VMEM((rows, feature_count), jnp.float32),
        ],
        compiler_params=pltpu.CompilerParams(vmem_limit_bytes=60 * 1024 * 1024),
    )(
        pltpu.with_memory_space_constraint(tokens, pltpu.MemorySpace.VMEM),
        gate_block,
        up_block,
        down_block,
        *[pltpu.with_memory_space_constraint(part, pltpu.MemorySpace.VMEM) for part in extra],
    )


def normalize(scores, usable):
    masked = jnp.where(usable, scores, -jnp.inf)
    largest = jnp.max(masked, axis=-1, keepdims=True)
    powers = jnp.exp(masked - largest)
    return (powers / jnp.sum(powers, axis=-1, keepdims=True)).astype(jnp.bfloat16)


def attend(query_latent, query_rope, latent_cache, rope_cache, lengths):
    requests, head_count, latent = query_latent.shape
    context = latent_cache.shape[1]
    rope_query = query_rope.reshape(requests, head_count, -1)
    position = lax.broadcasted_iota(jnp.int32, (1, 1, context), 2)
    usable = position < lengths[:, None, None]
    block_width = min(128, context)
    blocks_live = (jnp.max(lengths) + block_width - 1) // block_width

    def score_block(counter, scores):
        block_start = counter * block_width
        latent_block = lax.dynamic_slice_in_dim(latent_cache, block_start, block_width, 1)
        rope_block = lax.dynamic_slice_in_dim(rope_cache, block_start, block_width, 2)
        block_scores = attention_scores(query_latent, rope_query, latent_block, rope_block)
        return lax.dynamic_update_slice_in_dim(scores, block_scores, block_start, 2)

    empty_scores = jnp.full((requests, head_count, context), -jnp.inf, jnp.float32)
    scores = lax.fori_loop(0, blocks_live, score_block, empty_scores)
    weights = normalize(scores, usable)

    def value_block(counter, accumulated):
        block_start = counter * block_width
        weight_block = lax.dynamic_slice_in_dim(weights, block_start, block_width, 2)
        latent_block = lax.dynamic_slice_in_dim(latent_cache, block_start, block_width, 1)
        return accumulated + jnp.einsum(
            "rht,rtc->rhc", weight_block, latent_block, preferred_element_type=jnp.float32
        )

    output = lax.fori_loop(
        0, blocks_live, value_block, jnp.zeros((requests, head_count, latent), jnp.float32)
    )
    return output.astype(jnp.bfloat16)


def shards(
    query_latent,
    query_rope,
    latent_cache,
    rope_cache,
    lengths,
    moe_input,
    routes,
    route_weight,
    gate_weight,
    up_weight,
    down_weight,
):
    attended = attend(query_latent, query_rope, latent_cache, rope_cache, lengths)
    feature_count = moe_input.shape[1]
    top = routes.shape[1]
    extra = 2 * top
    column = lax.broadcasted_iota(jnp.int32, (moe_input.shape[0], feature_count + extra), 1)
    wide_rows = jnp.pad(moe_input, ((0, 0), (0, extra)))
    wide_routes = jnp.pad(routes.astype(jnp.bfloat16), ((0, 0), (feature_count, top)))
    wide_weights = jnp.pad(route_weight.astype(jnp.bfloat16), ((0, 0), (feature_count + top, 0)))
    packed = jnp.where(
        column < feature_count,
        wide_rows,
        jnp.where(column < feature_count + top, wide_routes, wide_weights),
    )
    pool = lax.all_gather(packed, "dev", axis=0, tiled=True)
    pool_rows = pool[:, :feature_count]
    pool_routes = pool[:, feature_count : feature_count + top].astype(jnp.float32)
    pool_weights = pool[:, feature_count + top :]
    node_count = lax.axis_size("node")
    dev_count = lax.axis_size("dev")
    expert_half = lax.axis_index("dev") // (dev_count // E_NODE)
    pooled = pool_rows.shape[0]
    slot_count = pooled * pool_routes.shape[1] // (E_NODE * node_count)
    targets = (jnp.arange(node_count, dtype=jnp.int32) * E_NODE + expert_half).astype(jnp.float32)
    matches = pool_routes[:, :, None] == targets[None, None, :]
    chosen = jnp.sum(matches.astype(jnp.float32), axis=1)
    route_share = jnp.sum(
        jnp.where(matches, pool_weights[:, :, None].astype(jnp.float32), 0.0), axis=1
    )
    before = jnp.cumsum(chosen, axis=0) - chosen
    slot_index = jnp.arange(slot_count, dtype=jnp.float32).reshape(1, slot_count, 1)
    selection = (chosen.T[:, None, :] == 1) & (before.T[:, None, :] == slot_index)
    selection = selection.reshape(node_count * slot_count, pooled)
    selector = selection.astype(jnp.bfloat16)
    route_rows = jnp.repeat(route_share.T, slot_count, axis=0)
    weighted = (selection.astype(jnp.float32) * route_rows).astype(jnp.bfloat16)
    batched = selector.reshape(node_count, slot_count, pooled)
    outgoing = jnp.einsum(
        "nsp,npd->nsd",
        batched,
        jnp.broadcast_to(pool_rows[None], (node_count, pooled, feature_count)),
        preferred_element_type=jnp.float32,
    ).astype(jnp.bfloat16)
    arrived = lax.all_to_all(outgoing, "node", split_axis=0, concat_axis=0, tiled=True)
    produced = expert_slice(arrived, gate_weight, up_weight, down_weight, outgoing)
    returned = lax.all_to_all(produced, "node", split_axis=0, concat_axis=0, tiled=True)
    returned = returned.reshape(node_count * slot_count, feature_count)
    pool_sum = jnp.einsum("qp,qd->pd", weighted, returned, preferred_element_type=jnp.float32)
    if dev_count > 8:
        combined = lax.psum_scatter(pool_sum, "dev", scatter_dimension=0, tiled=True)
        return (attended, combined.astype(jnp.bfloat16))
    own = lax.axis_index("dev")
    if dev_count == 4 and pooled == 4:
        pairs = pool_sum.reshape(2, 2, feature_count)
        core = own % 2
        keep = jnp.where(core == 0, pairs[:, 0], pairs[:, 1])
        send = jnp.where(core == 0, pairs[:, 1], pairs[:, 0])
        halves = keep + lax.ppermute(send, "dev", [(i, i ^ 1) for i in range(4)])
        chip = own // 2
        keep = jnp.where(chip == 0, halves[:1], halves[1:])
        send = jnp.where(chip == 0, halves[1:], halves[:1])
        combined = keep + lax.ppermute(send, "dev", [(i, i ^ 2) for i in range(4)])
        return (attended, combined.astype(jnp.bfloat16))
    rows_per = pooled // dev_count
    combined = lax.dynamic_slice_in_dim(pool_sum, own * rows_per, rows_per, 0)
    for shift in range(1, dev_count):
        target = (own + shift) % dev_count
        outgoing_part = lax.dynamic_slice_in_dim(pool_sum, target * rows_per, rows_per, 0)
        combined = combined + lax.ppermute(
            outgoing_part, "dev", [(i, (i + shift) % dev_count) for i in range(dev_count)]
        )
    return (attended, combined.astype(jnp.bfloat16))


def solution(mesh):
    in_specs = (
        P(("grp", "node", "dev"), None, None),
        P(("grp", "node", "dev"), None),
        P(("grp", "node", "dev"), None, None),
        P(("grp", "node", "dev"), None, None),
        P(("grp", "node", "dev")),
        P(("grp", "node", "dev"), None),
        P(("grp", "node", "dev"), None),
        P(("grp", "node", "dev"), None),
        P(("node", "dev"), None, None),
        P(("node", "dev"), None, None),
        P(("node", "dev"), None, None),
    )
    out_specs = (P(("grp", "node", "dev"), None, None), P(("grp", "node", "dev"), None))
    return jax.shard_map(shards, mesh=mesh, in_specs=in_specs, out_specs=out_specs, check_vma=False)
```

```python
import math

import jax
import jax.numpy as jnp
from jax import lax
from jax.experimental import pallas as pl
from jax.experimental.pallas import tpu as pltpu
from jax.sharding import PartitionSpec as P

E_NODE = 2


score_scale = 1.0 / math.sqrt(192.0)


def attention_scores(query_latent, rope_query, latent_block, rope_block):
    latent_part = jnp.einsum(
        "rhc,rtc->rht", query_latent, latent_block, preferred_element_type=jnp.float32
    )
    rope_part = jnp.einsum(
        "rhk,rkt->rht", rope_query, rope_block, preferred_element_type=jnp.float32
    )
    return score_scale * (latent_part + rope_part)


def prefetch_down(down_block, anchor, rows):
    feature_count = down_block.shape[2]

    def kernel(down_hbm, anchor_ref, down_out, sem):
        del anchor_ref
        copy = pltpu.make_async_copy(down_hbm.at[0, pl.ds(0, rows), :], down_out, sem.at[0])
        copy.start()
        copy.wait()

    return pl.pallas_call(
        kernel,
        in_specs=[pl.BlockSpec(memory_space=pl.ANY)] * 2,
        out_specs=pl.BlockSpec(memory_space=pltpu.VMEM),
        out_shape=pltpu.VMEM((rows, feature_count), down_block.dtype),
        scratch_shapes=[pltpu.SemaphoreType.DMA((1,))],
    )(down_block, anchor)


def expert_slice(tokens, gate_block, up_block, down_block, anchor):
    peers, slots, feature_count = tokens.shape
    rows = peers * slots
    hidden_count = gate_block.shape[2]
    width = min(256, hidden_count)
    blocks = hidden_count // width
    early = width // 2 if width >= 256 else 0
    extra = [prefetch_down(down_block, anchor, early)] if early else []

    def kernel(x_ref, gate_hbm, up_hbm, down_hbm, *rest):
        if early:
            down_first, out_ref, gate_buf, up_buf, down_buf, sems, x_all, acc_ref = rest
        else:
            out_ref, gate_buf, up_buf, down_buf, sems, x_all, acc_ref = rest
        copies = []
        for block in range(blocks):
            window = pl.ds(block * width, width)
            gate_copy = pltpu.make_async_copy(gate_hbm.at[0, :, window], gate_buf.at[block], sems.at[0, block])
            up_copy = pltpu.make_async_copy(up_hbm.at[0, :, window], up_buf.at[block], sems.at[1, block])
            if early and block == 0:
                down_copy = pltpu.make_async_copy(
                    down_hbm.at[0, pl.ds(early, width - early), :],
                    down_buf.at[0, pl.ds(early, width - early), :],
                    sems.at[2, 0],
                )
            else:
                down_copy = pltpu.make_async_copy(down_hbm.at[0, window, :], down_buf.at[block], sems.at[2, block])
            gate_copy.start()
            up_copy.start()
            down_copy.start()
            copies.append((gate_copy, up_copy, down_copy))
        for peer in range(peers):
            x_all[peer * slots : (peer + 1) * slots, :] = x_ref[peer].astype(jnp.float32)
        x = x_all[...].astype(jnp.bfloat16)
        acc_ref[...] = jnp.zeros_like(acc_ref)
        for block in range(blocks):
            gate_copy, up_copy, down_copy = copies[block]
            gate_copy.wait()
            up_copy.wait()
            gate_sum = jnp.dot(x, gate_buf[block], preferred_element_type=jnp.float32)
            up_sum = jnp.dot(x, up_buf[block], preferred_element_type=jnp.float32)
            hidden = (gate_sum / (1.0 + jnp.exp(-gate_sum)) * up_sum).astype(jnp.bfloat16)
            down_copy.wait()
            if early and block == 0:
                acc_ref[...] += jnp.dot(hidden[:, :early], down_first[...], preferred_element_type=jnp.float32)
                acc_ref[...] += jnp.dot(
                    hidden[:, early:], down_buf[0, early:, :], preferred_element_type=jnp.float32
                )
            else:
                acc_ref[...] += jnp.dot(hidden, down_buf[block], preferred_element_type=jnp.float32)
        for peer in range(peers):
            out_ref[peer] = acc_ref[peer * slots : (peer + 1) * slots, :].astype(out_ref.dtype)

    return pl.pallas_call(
        kernel,
        in_specs=[pl.BlockSpec(memory_space=pltpu.VMEM)]
        + [pl.BlockSpec(memory_space=pl.ANY)] * 3
        + [pl.BlockSpec(memory_space=pltpu.VMEM)] * len(extra),
        out_specs=pl.BlockSpec(memory_space=pltpu.VMEM),
        out_shape=jax.ShapeDtypeStruct((peers, slots, feature_count), jnp.bfloat16),
        scratch_shapes=[
            pltpu.VMEM((blocks, feature_count, width), gate_block.dtype),
            pltpu.VMEM((blocks, feature_count, width), up_block.dtype),
            pltpu.VMEM((blocks, width, feature_count), down_block.dtype),
            pltpu.SemaphoreType.DMA((3, blocks)),
            pltpu.VMEM((rows, feature_count), jnp.float32),
            pltpu.VMEM((rows, feature_count), jnp.float32),
        ],
        compiler_params=pltpu.CompilerParams(vmem_limit_bytes=60 * 1024 * 1024),
    )(
        pltpu.with_memory_space_constraint(tokens, pltpu.MemorySpace.VMEM),
        gate_block,
        up_block,
        down_block,
        *[pltpu.with_memory_space_constraint(part, pltpu.MemorySpace.VMEM) for part in extra],
    )


def normalize(scores, usable):
    masked = jnp.where(usable, scores, -jnp.inf)
    largest = jnp.max(masked, axis=-1, keepdims=True)
    powers = jnp.exp(masked - largest)
    return (powers / jnp.sum(powers, axis=-1, keepdims=True)).astype(jnp.bfloat16)


def attend(query_latent, query_rope, latent_cache, rope_cache, lengths):
    requests, head_count, latent = query_latent.shape
    context = latent_cache.shape[1]
    rope_query = query_rope.reshape(requests, head_count, -1)
    position = lax.broadcasted_iota(jnp.int32, (1, 1, context), 2)
    usable = position < lengths[:, None, None]
    block_width = min(128, context)
    blocks_live = (jnp.max(lengths) + block_width - 1) // block_width

    def score_block(counter, scores):
        block_start = counter * block_width
        latent_block = lax.dynamic_slice_in_dim(latent_cache, block_start, block_width, 1)
        rope_block = lax.dynamic_slice_in_dim(rope_cache, block_start, block_width, 2)
        block_scores = attention_scores(query_latent, rope_query, latent_block, rope_block)
        return lax.dynamic_update_slice_in_dim(scores, block_scores, block_start, 2)

    empty_scores = jnp.full((requests, head_count, context), -jnp.inf, jnp.float32)
    scores = lax.fori_loop(0, blocks_live, score_block, empty_scores)
    weights = normalize(scores, usable)

    def value_block(counter, accumulated):
        block_start = counter * block_width
        weight_block = lax.dynamic_slice_in_dim(weights, block_start, block_width, 2)
        latent_block = lax.dynamic_slice_in_dim(latent_cache, block_start, block_width, 1)
        return accumulated + jnp.einsum(
            "rht,rtc->rhc", weight_block, latent_block, preferred_element_type=jnp.float32
        )

    output = lax.fori_loop(
        0, blocks_live, value_block, jnp.zeros((requests, head_count, latent), jnp.float32)
    )
    return output.astype(jnp.bfloat16)


def shards(
    query_latent,
    query_rope,
    latent_cache,
    rope_cache,
    lengths,
    moe_input,
    routes,
    route_weight,
    gate_weight,
    up_weight,
    down_weight,
):
    attended = attend(query_latent, query_rope, latent_cache, rope_cache, lengths)
    feature_count = moe_input.shape[1]
    top = routes.shape[1]
    extra = 2 * top
    column = lax.broadcasted_iota(jnp.int32, (moe_input.shape[0], feature_count + extra), 1)
    wide_rows = jnp.pad(moe_input, ((0, 0), (0, extra)))
    wide_routes = jnp.pad(routes.astype(jnp.bfloat16), ((0, 0), (feature_count, top)))
    wide_weights = jnp.pad(route_weight.astype(jnp.bfloat16), ((0, 0), (feature_count + top, 0)))
    packed = jnp.where(
        column < feature_count,
        wide_rows,
        jnp.where(column < feature_count + top, wide_routes, wide_weights),
    )
    pool = lax.all_gather(packed, "dev", axis=0, tiled=True)
    pool_rows = pool[:, :feature_count]
    pool_routes = pool[:, feature_count : feature_count + top].astype(jnp.float32)
    pool_weights = pool[:, feature_count + top :]
    node_count = lax.axis_size("node")
    dev_count = lax.axis_size("dev")
    expert_half = lax.axis_index("dev") // (dev_count // E_NODE)
    pooled = pool_rows.shape[0]
    slot_count = pooled * pool_routes.shape[1] // (E_NODE * node_count)
    targets = (jnp.arange(node_count, dtype=jnp.int32) * E_NODE + expert_half).astype(jnp.float32)
    matches = pool_routes[:, :, None] == targets[None, None, :]
    chosen = jnp.sum(matches.astype(jnp.float32), axis=1)
    route_share = jnp.sum(
        jnp.where(matches, pool_weights[:, :, None].astype(jnp.float32), 0.0), axis=1
    )
    before = jnp.cumsum(chosen, axis=0) - chosen
    slot_index = jnp.arange(slot_count, dtype=jnp.float32).reshape(1, slot_count, 1)
    selection = (chosen.T[:, None, :] == 1) & (before.T[:, None, :] == slot_index)
    selection = selection.reshape(node_count * slot_count, pooled)
    selector = selection.astype(jnp.bfloat16)
    route_rows = jnp.repeat(route_share.T, slot_count, axis=0)
    weighted = (selection.astype(jnp.float32) * route_rows).astype(jnp.bfloat16)
    outgoing = jnp.dot(selector, pool_rows, preferred_element_type=jnp.float32)
    outgoing = outgoing.astype(jnp.bfloat16).reshape(node_count, slot_count, feature_count)
    arrived = lax.all_to_all(outgoing, "node", split_axis=0, concat_axis=0, tiled=True)
    produced = expert_slice(arrived, gate_weight, up_weight, down_weight, outgoing)
    returned = lax.all_to_all(produced, "node", split_axis=0, concat_axis=0, tiled=True)
    returned = returned.reshape(node_count * slot_count, feature_count)
    pool_sum = jnp.einsum("qp,qd->pd", weighted, returned, preferred_element_type=jnp.float32)
    if dev_count > 8:
        combined = lax.psum_scatter(pool_sum, "dev", scatter_dimension=0, tiled=True)
        return (attended, combined.astype(jnp.bfloat16))
    own = lax.axis_index("dev")
    if dev_count == 2 * E_NODE + 4 and pooled == 4:
        pairs = pool_sum.reshape(2, 2, feature_count)
        core = own % 2
        keep = jnp.where(core == 0, pairs[:, 0], pairs[:, 1])
        send = jnp.where(core == 0, pairs[:, 1], pairs[:, 0])
        halves = keep + lax.ppermute(send, "dev", [(i, i ^ 1) for i in range(4)])
        chip = own // 2
        keep = jnp.where(chip == 0, halves[:1], halves[1:])
        send = jnp.where(chip == 0, halves[1:], halves[:1])
        combined = keep + lax.ppermute(send, "dev", [(i, i ^ 2) for i in range(4)])
        return (attended, combined.astype(jnp.bfloat16))
    rows_per = pooled // dev_count
    combined = lax.dynamic_slice_in_dim(pool_sum, own * rows_per, rows_per, 0)
    for shift in range(1, dev_count):
        target = (own + shift) % dev_count
        outgoing_part = lax.dynamic_slice_in_dim(pool_sum, target * rows_per, rows_per, 0)
        combined = combined + lax.ppermute(
            outgoing_part, "dev", [(i, (i + shift) % dev_count) for i in range(dev_count)]
        )
    return (attended, combined.astype(jnp.bfloat16))


def solution(mesh):
    in_specs = (
        P(("grp", "node", "dev"), None, None),
        P(("grp", "node", "dev"), None),
        P(("grp", "node", "dev"), None, None),
        P(("grp", "node", "dev"), None, None),
        P(("grp", "node", "dev")),
        P(("grp", "node", "dev"), None),
        P(("grp", "node", "dev"), None),
        P(("grp", "node", "dev"), None),
        P(("node", "dev"), None, None),
        P(("node", "dev"), None, None),
        P(("node", "dev"), None, None),
    )
    out_specs = (P(("grp", "node", "dev"), None, None), P(("grp", "node", "dev"), None))
    return jax.shard_map(shards, mesh=mesh, in_specs=in_specs, out_specs=out_specs, check_vma=False)
```
